128 devices in a mesh: sec: 2 (over z_hi), row: 8 (over z_lo, y), col: 8 (over x, core).
Axes of the slice: x: 4, y: 4, z: 4 (z_hi: 2, z_lo: 2; z = z_hi * 2 + z_lo), core: 2. Of those that a mesh axis runs over, the one named last changes fastest.
Arguments:
- left_feat: bfloat16 [320, 16, 2048], P(None, 'row', 'col'), may hold values from -8 to 8
- right_feat: bfloat16 [320, 16, 2048], P(None, 'row', 'col'), may hold values from -8 to 8
- offsets: int32 [8, 8], P('row', 'col'), may hold values from 0 to 79, as said below
- w_first: bfloat16 [32, 40, 3, 3, 3], replicated, may hold values from -0.1875 to 0.1875
- b_first: float32 [32], replicated, may hold values from -3 to 3
- w_second: bfloat16 [32, 32, 3, 3, 3], replicated, may hold values from -0.21875 to 0.21875
- b_second: float32 [32], replicated, may hold values from -3 to 3
- w_third: bfloat16 [32, 32, 3, 3, 3], replicated, may hold values from -0.21875 to 0.21875
- b_third: float32 [32], replicated, may hold values from -3 to 3
- w_out: bfloat16 [1, 32, 3, 3, 3], replicated, may hold values from -0.21875 to 0.21875
- b_out: float32 [1], replicated, may hold values from -3 to 3
Outputs:
- cost: float32 [48, 16, 2048], P('sec', 'row', 'col')
The draws below stay inside these ranges and needn't reach their ends.
Inputs may be any that keep to these rules, and one draw needn't show every extreme that they name: `offsets`: one offset a tile; some tile has offset 0 and some tile has offset 80 - 1.
All inputs are finite; a program needn't handle non-finite values.
Results may differ from the reference program's by a relative error of at most 0.006.
Values may be sent and summed in bfloat16 or wider, within the bound.
No kernel may reach another device: no remote copies, remote signals or barrier semaphores. Data moves between devices by JAX's collectives and lax.ppermute only.
A program may use at most 128 MiB of HBM per device.

```python
import jax
import jax.numpy as jnp
from jax import lax

C = 320
G = 40
F = 32
DISP = 48
OFF_SPAN = 80
TH = 2
TW = 256
H = 16
W = 2048
STRIP = 128
GS = 8
N_ROW = 8
N_COL = 8


def draw_offsets(key, part):
    key_base, key_high, key_low = jax.random.split(jax.random.fold_in(key, 17), 3)
    count = N_ROW * N_COL
    values = jax.random.randint(key_base, (count,), 0, OFF_SPAN, dtype=jnp.int32)
    high_pos = jax.random.randint(key_high, (), 0, count, dtype=jnp.int32)
    step_low = jax.random.randint(key_low, (), 1, count, dtype=jnp.int32)
    low_pos = (high_pos + step_low) % count
    values = values.at[high_pos].set(OFF_SPAN - 1)
    values = values.at[low_pos].set(0)
    return values.reshape(N_ROW, N_COL)


def block_scale(own_key, shape, cuts, smallest, largest):
    gain, own = 1.0, jax.random.fold_in(own_key, 6)
    for position, shards_of in cuts:
        draws = jnp.exp(jax.random.uniform(jax.random.fold_in(own, position), (shards_of,), jnp.float32, smallest / len(cuts), largest / len(cuts)))
        gain = gain * jnp.repeat(draws, shape[position] // shards_of).reshape([-1 if axis == position else 1 for axis in range(len(shape))])
    return gain


def noise(key, extent, spread, bound, pieces=(), kind=jnp.bfloat16):
    array = jax.random.normal(key, extent, jnp.float32) * spread
    if len(pieces) > 0:
        array = block_scale(key, extent, pieces, -0.22, 0.18) * array
    return jnp.clip(array, min=-bound, max=bound).astype(kind)


def setup_inputs(seed: int = 0) -> dict:
    arg_keys = jax.random.split(jax.random.key(seed), 12)
    return {
        "left_feat": noise(arg_keys[0], (C, H, W), 1.5, 8.0, ((1, 8), (2, 8))),
        "right_feat": noise(arg_keys[1], (C, H, W), 1.5, 8.0, ((1, 8), (2, 8))),
        "offsets": draw_offsets(jax.random.fold_in(arg_keys[11], 71), 0),
        "w_first": noise(arg_keys[3], (F, G, 3, 3, 3), (27 * G) ** -0.5, 0.1875),
        "b_first": noise(arg_keys[4], (F,), 0.5, 3.0, (), jnp.float32),
        "w_second": noise(arg_keys[5], (F, F, 3, 3, 3), (27 * F) ** -0.5, 0.21875),
        "b_second": noise(arg_keys[6], (F,), 0.5, 3.0, (), jnp.float32),
        "w_third": noise(arg_keys[7], (F, F, 3, 3, 3), (27 * F) ** -0.5, 0.21875),
        "b_third": noise(arg_keys[8], (F,), 0.5, 3.0, (), jnp.float32),
        "w_out": noise(arg_keys[9], (1, F, 3, 3, 3), (27 * F) ** -0.5, 0.21875),
        "b_out": noise(arg_keys[10], (1,), 0.5, 3.0, (), jnp.float32),
    }


def conv_three(volume, kernel):
    padded = jnp.pad(volume, ((0, 0), (1, 1), (1, 1), (1, 1)))
    result = lax.conv_general_dilated(padded[None], kernel, (1, 1, 1), "VALID", dimension_numbers=("NCDHW", "OIDHW", "NCDHW"), preferred_element_type=jnp.float32)
    return result[0]


def reference(left_feat, right_feat, offsets, w_first, b_first, w_second, b_second, w_third, b_third, w_out, b_out):
    shift_map = jnp.repeat(jnp.repeat(offsets, TH, axis=0), TW, axis=1).astype(jnp.int32)
    right_pad = jnp.pad(right_feat, ((0, 0), (0, 0), (STRIP, 0)))
    columns = jnp.arange(W, dtype=jnp.int32)[None, :]

    def one_level(level):
        index = columns - shift_map - level + STRIP
        index = jnp.broadcast_to(index[None], (C, H, W)).astype(jnp.int32)
        moved = jnp.take_along_axis(right_pad, index, axis=2)
        product = left_feat.astype(jnp.float32) * moved.astype(jnp.float32)
        return (product.reshape(G, GS, H, W).sum(axis=1) / GS).astype(jnp.bfloat16)

    corr = lax.map(one_level, jnp.arange(DISP, dtype=jnp.int32))
    corr = jnp.transpose(corr, (1, 0, 2, 3))
    act_one = jax.nn.relu(conv_three(corr, w_first) + b_first[:, None, None, None]).astype(jnp.bfloat16)
    act_two = jax.nn.relu(conv_three(act_one, w_second) + b_second[:, None, None, None]).astype(jnp.bfloat16)
    act_three = jax.nn.relu(conv_three(act_two, w_third) + b_third[:, None, None, None] + act_one.astype(jnp.float32)).astype(jnp.bfloat16)
    cost = conv_three(act_three, w_out) + b_out[:, None, None, None]
    return cost[0]
```

```python
import jax
import jax.numpy as jnp
from jax import lax
from jax.experimental import pallas as pl
from jax.sharding import PartitionSpec as P

G = 40
DISP = 48
GS = 8
EXT = 4
PRE = 136


def from_behind(array, axis, by):
    size = lax.axis_size(axis)
    pairs = [(i, i + by) for i in range(size) if 0 <= i + by < size]
    return lax.ppermute(array, axis, pairs)


def row_halo(cells):
    above = from_behind(cells[:, :, -1:], "row", 1)
    below = from_behind(cells[:, :, :1], "row", -1)
    return jnp.concatenate([above, cells, below], axis=2)


def inside(levels, width, ext):
    first_level = lax.axis_index("sec") * (DISP // lax.axis_size("sec"))
    first_col = lax.axis_index("col") * (width - 2 * ext)
    total = (width - 2 * ext) * lax.axis_size("col")
    level = first_level - ext + jnp.arange(levels)
    col = first_col - ext + jnp.arange(width)
    keep_level = (level >= 0) & (level < DISP)
    keep_col = (col >= 0) & (col < total)
    return keep_level[:, None, None] & keep_col[None, None, :]


def conv3(volume, kernel):
    out = lax.conv_general_dilated(
        volume[None],
        kernel,
        (1, 1, 1),
        "VALID",
        dimension_numbers=("NCDHW", "OIDHW", "NCDHW"),
        preferred_element_type=jnp.float32,
    )
    return out[0]


def correlate_kernel(left_ref, window_ref, out_ref):
    rows, _, width = left_ref.shape
    count = out_ref.shape[1]
    for row in range(rows):
        left = left_ref[row].astype(jnp.float32)
        window = window_ref[row].astype(jnp.float32)
        for level in range(count):
            begin = count - 1 - level
            product = left * window[:, begin : begin + width]
            summed = product.reshape(G, GS, width).sum(axis=1)
            out_ref[row, level] = (summed / GS).astype(jnp.bfloat16)


def correlate(left, window, count, width):
    chans, rows, _ = left.shape
    out = pl.pallas_call(
        correlate_kernel,
        out_shape=jax.ShapeDtypeStruct((rows, count, G, width), jnp.bfloat16),
    )(jnp.transpose(left, (1, 0, 2)), jnp.transpose(window, (1, 0, 2)))
    return jnp.transpose(out, (2, 1, 0, 3))


def layer(volume, kernel, bias, ext, extra=None):
    out = conv3(row_halo(volume), kernel) + bias[:, None, None, None]
    if extra is not None:
        out = out + extra
    out = jax.nn.relu(out)
    keep = inside(out.shape[1], out.shape[3], ext)
    return jnp.where(keep, out, 0.0).astype(jnp.bfloat16)


def shards(
    left_feat,
    right_feat,
    offsets,
    w_first,
    b_first,
    w_second,
    b_second,
    w_third,
    b_third,
    w_out,
    b_out,
):
    chans, rows, width = left_feat.shape
    levels = DISP // lax.axis_size("sec")
    count = levels + 2 * EXT
    first_level = lax.axis_index("sec") * levels
    own_shift = offsets[0, 0]
    left_shift = from_behind(offsets, "col", 1)[0, 0]
    right_shift = from_behind(offsets, "col", -1)[0, 0]
    right_ext = jnp.concatenate(
        [
            from_behind(right_feat[:, :, width - PRE :], "col", 1),
            right_feat,
            from_behind(right_feat[:, :, : 2 * EXT], "col", -1),
        ],
        axis=2,
    )
    left_ext = jnp.concatenate(
        [
            from_behind(left_feat[:, :, width - EXT :], "col", 1),
            left_feat,
            from_behind(left_feat[:, :, :EXT], "col", -1),
        ],
        axis=2,
    )
    pieces = []
    for begin, span, shift in ((-EXT, EXT, left_shift), (0, width, own_shift), (width, EXT, right_shift)):
        start = PRE + begin - shift - first_level + EXT - (count - 1)
        window = lax.dynamic_slice_in_dim(right_ext, start, span + count - 1, axis=2)
        own_left = left_ext[:, :, EXT + begin : EXT + begin + span]
        pieces.append(correlate(own_left, window, count, span))
    corr = jnp.concatenate(pieces, axis=3)
    corr = jnp.where(inside(count, width + 2 * EXT, EXT), corr, 0.0).astype(jnp.bfloat16)

    act_one = layer(corr, w_first, b_first, EXT - 1)
    act_two = layer(act_one, w_second, b_second, EXT - 2)
    act_three = layer(
        act_two, w_third, b_third, EXT - 3, extra=act_one[:, 2:-2, :, 2:-2].astype(jnp.float32)
    )
    cost = conv3(row_halo(act_three), w_out) + b_out[:, None, None, None]
    return cost[0]


def solution(mesh):
    return jax.shard_map(
        shards,
        mesh=mesh,
        in_specs=(
            P(None, "row", "col"),
            P(None, "row", "col"),
            P("row", "col"),
            P(),
            P(),
            P(),
            P(),
            P(),
            P(),
            P(),
            P(),
        ),
        out_specs=P("sec", "row", "col"),
        check_vma=False,
    )
```

```python
import functools

import jax
import jax.numpy as jnp
from jax import lax
from jax.experimental import pallas as pl
from jax.sharding import PartitionSpec as P

G = 40
DISP = 48
GS = 8
EXT = 4
PRE = 136
LINE = 384
DEPTH = 34
STEP = 1536


def from_behind(array, axis, by):
    size = lax.axis_size(axis)
    pairs = [(i, i + by) for i in range(size) if 0 <= i + by < size]
    return lax.ppermute(array, axis, pairs)


def row_halo(cells):
    above = from_behind(cells[:, :, -1:], "row", 1)
    below = from_behind(cells[:, :, :1], "row", -1)
    return jnp.concatenate([above, cells, below], axis=2)


def inside(levels, width, ext):
    first_level = lax.axis_index("sec") * (DISP // lax.axis_size("sec"))
    first_col = lax.axis_index("col") * (width - 2 * ext)
    total = (width - 2 * ext) * lax.axis_size("col")
    level = first_level - ext + jnp.arange(levels)
    col = first_col - ext + jnp.arange(width)
    keep_level = (level >= 0) & (level < DISP)
    keep_col = (col >= 0) & (col < total)
    return keep_level[:, None, None] & keep_col[None, None, :]


def conv3(volume, kernel):
    out = lax.conv_general_dilated(
        volume[None],
        kernel,
        (1, 1, 1),
        "VALID",
        dimension_numbers=("NCDHW", "OIDHW", "NCDHW"),
        preferred_element_type=jnp.float32,
    )
    return out[0]


def correlate_kernel(left_ref, window_ref, out_ref):
    rows, _, width = left_ref.shape
    count = out_ref.shape[1]
    for row in range(rows):
        left = left_ref[row].astype(jnp.float32)
        window = window_ref[row].astype(jnp.float32)
        for level in range(count):
            begin = count - 1 - level
            product = left * window[:, begin : begin + width]
            summed = product.reshape(G, GS, width).sum(axis=1)
            out_ref[row, level] = (summed / GS).astype(jnp.bfloat16)


def correlate(left, window, count, width):
    chans, rows, _ = left.shape
    out = pl.pallas_call(
        correlate_kernel,
        out_shape=jax.ShapeDtypeStruct((rows, count, G, width), jnp.bfloat16),
    )(jnp.transpose(left, (1, 0, 2)), jnp.transpose(window, (1, 0, 2)))
    return jnp.transpose(out, (2, 1, 0, 3))


def conv_kernel(x_ref, w_ref, b_ref, keep_ref, *rest, cout, relu, shifts):
    if len(rest) == 2:
        extra_ref, o_ref = rest
    else:
        extra_ref = None
        (o_ref,) = rest
    total = o_ref.shape[1]
    for base in range(0, total, STEP):
        stacked = jnp.concatenate(
            [x_ref[:, base + shift : base + shift + STEP + 128] for shift in shifts], axis=0
        )
        z = jnp.dot(w_ref[...], stacked, preferred_element_type=jnp.float32)
        out = z[0:cout, 0:STEP] + z[cout : 2 * cout, 1 : STEP + 1]
        out = out + z[2 * cout : 3 * cout, 2 : STEP + 2]
        out = out + b_ref[...]
        if extra_ref is not None:
            out = out + extra_ref[:, base : base + STEP].astype(jnp.float32)
        if relu:
            out = jnp.maximum(out, 0.0)
        out = jnp.where(keep_ref[:, base : base + STEP] > 0, out, 0.0)
        o_ref[:, base : base + STEP] = out.astype(o_ref.dtype)


def keep_lines(levels, cols, ext):
    first_level = lax.axis_index("sec") * (DISP // lax.axis_size("sec"))
    width = cols - 2 * ext
    first_col = lax.axis_index("col") * width
    total = width * lax.axis_size("col")
    level = first_level - ext + jnp.arange(DEPTH)
    col = first_col - ext + jnp.arange(LINE)
    keep_level = (level >= 0) & (level < DISP) & (jnp.arange(DEPTH) < levels)
    keep_col = (col >= 0) & (col < total) & (jnp.arange(LINE) < cols)
    return keep_level[:, None] & keep_col[None, :]


def conv_layer(planes, kernel, bias, keep, extra=None, relu=True, out_dtype=jnp.bfloat16):
    chans = planes.shape[0]
    cout, cin = kernel.shape[:2]
    rows_out = max(cout, 8)
    taps = jnp.transpose(kernel, (4, 0, 2, 3, 1))
    taps = jnp.pad(taps, ((0, 0), (0, rows_out - cout), (0, 0), (0, 0), (0, chans - cin)))
    taps = taps.reshape(3 * rows_out, 9 * chans)
    bias_col = jnp.pad(bias, (0, rows_out - cout)).reshape(rows_out, 1)
    total = 2 * DEPTH * LINE
    shifts = tuple(b * DEPTH * LINE + a * LINE for a in range(3) for b in range(3))
    need = total + max(shifts) + 128
    planes = jnp.pad(planes, ((0, 0), (0, need - planes.shape[1])))
    operands = [planes, taps, bias_col, keep]
    if extra is not None:
        operands.append(extra)
    out = pl.pallas_call(
        functools.partial(conv_kernel, cout=rows_out, relu=relu, shifts=shifts),
        out_shape=jax.ShapeDtypeStruct((rows_out, total), out_dtype),
    )(*operands)
    return out[:cout]


def with_rows(own, levels, cols):
    chans = own.shape[0]
    pad = ((0, 0), (0, 0), (0, DEPTH - levels), (0, LINE - cols))
    above = jnp.pad(from_behind(own[:, 1:, :levels, :cols], "row", 1), pad)
    below = jnp.pad(from_behind(own[:, :1, :levels, :cols], "row", -1), pad)
    return jnp.concatenate([above, own, below], axis=1).reshape(chans, 4 * DEPTH * LINE)


def shards(
    left_feat,
    right_feat,
    offsets,
    w_first,
    b_first,
    w_second,
    b_second,
    w_third,
    b_third,
    w_out,
    b_out,
):
    chans, rows, width = left_feat.shape
    levels = DISP // lax.axis_size("sec")
    count = levels + 2 * EXT
    first_level = lax.axis_index("sec") * levels
    own_shift = offsets[0, 0]
    left_shift = from_behind(offsets, "col", 1)[0, 0]
    right_shift = from_behind(offsets, "col", -1)[0, 0]
    right_ext = jnp.concatenate(
        [
            from_behind(right_feat[:, :, width - PRE :], "col", 1),
            right_feat,
            from_behind(right_feat[:, :, : 2 * EXT], "col", -1),
        ],
        axis=2,
    )
    left_ext = jnp.concatenate(
        [
            from_behind(left_feat[:, :, width - EXT :], "col", 1),
            left_feat,
            from_behind(left_feat[:, :, :EXT], "col", -1),
        ],
        axis=2,
    )
    pieces = []
    for begin, span, shift in ((-EXT, EXT, left_shift), (0, width, own_shift), (width, EXT, right_shift)):
        start = PRE + begin - shift - first_level + EXT - (count - 1)
        window = lax.dynamic_slice_in_dim(right_ext, start, span + count - 1, axis=2)
        own_left = left_ext[:, :, EXT + begin : EXT + begin + span]
        pieces.append(correlate(own_left, window, count, span))
    corr = jnp.concatenate(pieces, axis=3)
    count_cols = width + 2 * EXT
    corr = jnp.transpose(corr, (0, 2, 1, 3))
    chans_in = -(-G // 16) * 16
    corr = jnp.pad(
        corr, ((0, chans_in - G), (0, 0), (0, DEPTH - count), (0, LINE - count_cols))
    )
    corr = jnp.where(keep_lines(count, count_cols, EXT), corr, 0.0).astype(jnp.bfloat16)

    sizes = [(count - 2 * k, count_cols - 2 * k) for k in range(EXT + 1)]
    flat = 2 * DEPTH * LINE

    def keep_of(k):
        return keep_lines(sizes[k][0], sizes[k][1], EXT - k)[None].repeat(2, 0).reshape(1, flat)

    act_one = conv_layer(with_rows(corr, *sizes[0]), w_first, b_first, keep_of(1))
    act_one = act_one.reshape(-1, 2, DEPTH, LINE)
    act_two = conv_layer(with_rows(act_one, *sizes[1]), w_second, b_second, keep_of(2))
    act_two = act_two.reshape(-1, 2, DEPTH, LINE)
    residual = jnp.pad(act_one[:, :, 2:, 2:], ((0, 0), (0, 0), (0, 2), (0, 2))).reshape(-1, flat)
    act_three = conv_layer(
        with_rows(act_two, *sizes[2]), w_third, b_third, keep_of(3), extra=residual
    )
    act_three = act_three.reshape(-1, 2, DEPTH, LINE)
    everywhere = jnp.ones((1, flat), jnp.float32)
    cost = conv_layer(
        with_rows(act_three, *sizes[3]), w_out, b_out, everywhere, relu=False,
        out_dtype=jnp.float32,
    )
    cost = cost.reshape(2, DEPTH, LINE)[:, :levels, :width]
    return jnp.transpose(cost, (1, 0, 2))


def solution(mesh):
    return jax.shard_map(
        shards,
        mesh=mesh,
        in_specs=(
            P(None, "row", "col"),
            P(None, "row", "col"),
            P("row", "col"),
            P(),
            P(),
            P(),
            P(),
            P(),
            P(),
            P(),
            P(),
        ),
        out_specs=P("sec", "row", "col"),
        check_vma=False,
    )
```

```python
import functools

import jax
import jax.numpy as jnp
from jax import lax
from jax.experimental import pallas as pl
from jax.sharding import PartitionSpec as P

G = 40
DISP = 48
GS = 8
EXT = 4
PRE = 136
LINE = 384
DEPTH = 32
STEP = 1536


def from_behind(array, axis, by):
    size = lax.axis_size(axis)
    pairs = [(i, i + by) for i in range(size) if 0 <= i + by < size]
    return lax.ppermute(array, axis, pairs)


def row_halo(cells):
    above = from_behind(cells[:, :, -1:], "row", 1)
    below = from_behind(cells[:, :, :1], "row", -1)
    return jnp.concatenate([above, cells, below], axis=2)


def inside(levels, width, ext):
    first_level = lax.axis_index("sec") * (DISP // lax.axis_size("sec"))
    first_col = lax.axis_index("col") * (width - 2 * ext)
    total = (width - 2 * ext) * lax.axis_size("col")
    level = first_level - ext + jnp.arange(levels)
    col = first_col - ext + jnp.arange(width)
    keep_level = (level >= 0) & (level < DISP)
    keep_col = (col >= 0) & (col < total)
    return keep_level[:, None, None] & keep_col[None, None, :]


def conv3(volume, kernel):
    out = lax.conv_general_dilated(
        volume[None],
        kernel,
        (1, 1, 1),
        "VALID",
        dimension_numbers=("NCDHW", "OIDHW", "NCDHW"),
        preferred_element_type=jnp.float32,
    )
    return out[0]


def correlate_kernel(left_ref, window_ref, out_ref):
    rows, _, width = left_ref.shape
    count = out_ref.shape[1]
    for row in range(rows):
        left = left_ref[row].astype(jnp.float32)
        window = window_ref[row].astype(jnp.float32)
        for level in range(count):
            begin = count - 1 - level
            product = left * window[:, begin : begin + width]
            summed = product.reshape(G, GS, width).sum(axis=1)
            out_ref[row, level] = (summed / GS).astype(jnp.bfloat16)


def correlate(left, window, count, width):
    chans, rows, _ = left.shape
    out = pl.pallas_call(
        correlate_kernel,
        out_shape=jax.ShapeDtypeStruct((rows, count, G, width), jnp.bfloat16),
    )(jnp.transpose(left, (1, 0, 2)), jnp.transpose(window, (1, 0, 2)))
    return jnp.transpose(out, (2, 1, 0, 3))


def conv_kernel(x_ref, w_ref, b_ref, keep_ref, *rest, cout, relu, shifts):
    if len(rest) == 2:
        extra_ref, o_ref = rest
    else:
        extra_ref = None
        (o_ref,) = rest
    total = o_ref.shape[1]
    for base in range(0, total, STEP):
        stacked = jnp.concatenate(
            [x_ref[:, base + shift : base + shift + STEP + 128] for shift in shifts], axis=0
        )
        z = jnp.dot(w_ref[...], stacked, preferred_element_type=jnp.float32)
        out = z[0:cout, 0:STEP] + z[cout : 2 * cout, 1 : STEP + 1]
        out = out + z[2 * cout : 3 * cout, 2 : STEP + 2]
        out = out + b_ref[...]
        if extra_ref is not None:
            out = out + extra_ref[:, base : base + STEP].astype(jnp.float32)
        if relu:
            out = jnp.maximum(out, 0.0)
        out = jnp.where(keep_ref[:, base : base + STEP] > 0, out, 0.0)
        o_ref[:, base : base + STEP] = out.astype(o_ref.dtype)


def keep_lines(levels, cols, ext):
    first_level = lax.axis_index("sec") * (DISP // lax.axis_size("sec"))
    width = cols - 2 * ext
    first_col = lax.axis_index("col") * width
    total = width * lax.axis_size("col")
    level = first_level - ext + jnp.arange(DEPTH)
    col = first_col - ext + jnp.arange(LINE)
    keep_level = (level >= 0) & (level < DISP) & (jnp.arange(DEPTH) < levels)
    keep_col = (col >= 0) & (col < total) & (jnp.arange(LINE) < cols)
    return keep_level[:, None] & keep_col[None, :]


def conv_layer(planes, kernel, bias, keep, extra=None, relu=True, out_dtype=jnp.bfloat16):
    chans = planes.shape[0]
    cout, cin = kernel.shape[:2]
    rows_out = max(cout, 8)
    taps = jnp.transpose(kernel, (4, 0, 2, 3, 1))
    taps = jnp.pad(taps, ((0, 0), (0, rows_out - cout), (0, 0), (0, 0), (0, chans - cin)))
    taps = taps.reshape(3 * rows_out, 9 * chans)
    bias_col = jnp.pad(bias, (0, rows_out - cout)).reshape(rows_out, 1)
    total = 2 * DEPTH * LINE
    shifts = tuple(b * DEPTH * LINE + a * LINE for a in range(3) for b in range(3))
    assert planes.shape[1] == total + max(shifts) + 128
    operands = [planes, taps, bias_col, keep]
    if extra is not None:
        operands.append(extra)
    out = pl.pallas_call(
        functools.partial(conv_kernel, cout=rows_out, relu=relu, shifts=shifts),
        out_shape=jax.ShapeDtypeStruct((rows_out, total), out_dtype),
    )(*operands)
    return out[:cout]


def with_rows(own, levels, cols, sent):
    chans = own.shape[0]
    pad = ((0, chans - sent), (0, 0), (0, DEPTH - levels), (0, LINE - cols))
    above = jnp.pad(from_behind(own[:sent, 1:, :levels, :cols], "row", 1), pad)
    below = jnp.pad(from_behind(own[:sent, :1, :levels, :cols], "row", -1), pad)
    tail = jnp.zeros((chans, 2 * LINE + 128), own.dtype)
    parts = [above, own, below]
    return jnp.concatenate([part.reshape(chans, -1) for part in parts] + [tail], axis=1)


def shards(
    left_feat,
    right_feat,
    offsets,
    w_first,
    b_first,
    w_second,
    b_second,
    w_third,
    b_third,
    w_out,
    b_out,
):
    chans, rows, width = left_feat.shape
    levels = DISP // lax.axis_size("sec")
    count = levels + 2 * EXT
    first_level = lax.axis_index("sec") * levels
    own_shift = offsets[0, 0]
    left_shift = from_behind(offsets, "col", 1)[0, 0]
    right_shift = from_behind(offsets, "col", -1)[0, 0]
    right_ext = jnp.concatenate(
        [
            from_behind(right_feat[:, :, width - PRE :], "col", 1),
            right_feat,
            from_behind(right_feat[:, :, : 2 * EXT], "col", -1),
        ],
        axis=2,
    )
    left_ext = jnp.concatenate(
        [
            from_behind(left_feat[:, :, width - EXT :], "col", 1),
            left_feat,
            from_behind(left_feat[:, :, :EXT], "col", -1),
        ],
        axis=2,
    )
    pieces = []
    for begin, span, shift in ((-EXT, EXT, left_shift), (0, width, own_shift), (width, EXT, right_shift)):
        start = PRE + begin - shift - first_level + EXT - (count - 1)
        window = lax.dynamic_slice_in_dim(right_ext, start, span + count - 1, axis=2)
        own_left = left_ext[:, :, EXT + begin : EXT + begin + span]
        pieces.append(correlate(own_left, window, count, span))
    corr = jnp.concatenate(pieces, axis=3)
    count_cols = width + 2 * EXT
    corr = jnp.transpose(corr, (0, 2, 1, 3))
    chans_in = -(-G // 16) * 16
    corr = jnp.pad(
        corr, ((0, chans_in - G), (0, 0), (0, DEPTH - count), (0, LINE - count_cols))
    )
    corr = jnp.where(keep_lines(count, count_cols, EXT), corr, 0.0).astype(jnp.bfloat16)

    sizes = [(count - 2 * k, count_cols - 2 * k) for k in range(EXT + 1)]
    flat = 2 * DEPTH * LINE

    def keep_of(k):
        return keep_lines(sizes[k][0], sizes[k][1], EXT - k)[None].repeat(2, 0).reshape(1, flat)

    act_one = conv_layer(with_rows(corr, *sizes[0], G), w_first, b_first, keep_of(1))
    act_one = act_one.reshape(-1, 2, DEPTH, LINE)
    act_two = conv_layer(with_rows(act_one, *sizes[1], act_one.shape[0]), w_second, b_second, keep_of(2))
    act_two = act_two.reshape(-1, 2, DEPTH, LINE)
    residual = jnp.pad(act_one[:, :, 2:, 2:], ((0, 0), (0, 0), (0, 2), (0, 2))).reshape(-1, flat)
    act_three = conv_layer(
        with_rows(act_two, *sizes[2], act_two.shape[0]), w_third, b_third, keep_of(3), extra=residual
    )
    act_three = act_three.reshape(-1, 2, DEPTH, LINE)
    everywhere = jnp.ones((1, flat), jnp.float32)
    cost = conv_layer(
        with_rows(act_three, *sizes[3], act_three.shape[0]), w_out, b_out, everywhere, relu=False,
        out_dtype=jnp.float32,
    )
    cost = cost.reshape(2, DEPTH, LINE)[:, :levels, :width]
    return jnp.transpose(cost, (1, 0, 2))


def solution(mesh):
    return jax.shard_map(
        shards,
        mesh=mesh,
        in_specs=(
            P(None, "row", "col"),
            P(None, "row", "col"),
            P("row", "col"),
            P(),
            P(),
            P(),
            P(),
            P(),
            P(),
            P(),
            P(),
        ),
        out_specs=P("sec", "row", "col"),
        check_vma=False,
    )
```

```python
import functools

import jax
import jax.numpy as jnp
from jax import lax
from jax.experimental import pallas as pl
from jax.sharding import PartitionSpec as P

G = 40
DISP = 48
GS = 8
EXT = 4
PRE = 136
LINE = 384
DEPTH = 32
STEP = 1536


def from_behind(array, axis, by):
    size = lax.axis_size(axis)
    pairs = [(i, i + by) for i in range(size) if 0 <= i + by < size]
    return lax.ppermute(array, axis, pairs)


def row_halo(cells):
    above = from_behind(cells[:, :, -1:], "row", 1)
    below = from_behind(cells[:, :, :1], "row", -1)
    return jnp.concatenate([above, cells, below], axis=2)


def inside(levels, width, ext):
    first_level = lax.axis_index("sec") * (DISP // lax.axis_size("sec"))
    first_col = lax.axis_index("col") * (width - 2 * ext)
    total = (width - 2 * ext) * lax.axis_size("col")
    level = first_level - ext + jnp.arange(levels)
    col = first_col - ext + jnp.arange(width)
    keep_level = (level >= 0) & (level < DISP)
    keep_col = (col >= 0) & (col < total)
    return keep_level[:, None, None] & keep_col[None, None, :]


def conv3(volume, kernel):
    out = lax.conv_general_dilated(
        volume[None],
        kernel,
        (1, 1, 1),
        "VALID",
        dimension_numbers=("NCDHW", "OIDHW", "NCDHW"),
        preferred_element_type=jnp.float32,
    )
    return out[0]


def correlate_kernel(left_ref, window_ref, out_ref):
    rows, _, width = left_ref.shape
    count = out_ref.shape[1]
    for row in range(rows):
        left = left_ref[row].astype(jnp.float32)
        window = window_ref[row].astype(jnp.float32)
        for level in range(count):
            begin = count - 1 - level
            product = left * window[:, begin : begin + width]
            summed = product.reshape(G, GS, width).sum(axis=1)
            out_ref[row, level] = (summed / GS).astype(jnp.bfloat16)


def correlate(left, window, count, width):
    chans, rows, _ = left.shape
    out = pl.pallas_call(
        correlate_kernel,
        out_shape=jax.ShapeDtypeStruct((rows, count, G, width), jnp.bfloat16),
    )(jnp.transpose(left, (1, 0, 2)), jnp.transpose(window, (1, 0, 2)))
    return jnp.transpose(out, (2, 1, 0, 3))


def conv_kernel(x_ref, w_ref, b_ref, keep_ref, *rest, cout, relu, shifts):
    if len(rest) == 2:
        extra_ref, o_ref = rest
    else:
        extra_ref = None
        (o_ref,) = rest
    total = o_ref.shape[1]
    for base in range(0, total, STEP):
        stacked = jnp.concatenate(
            [x_ref[:, base + shift : base + shift + STEP + 128] for shift in shifts], axis=0
        )
        z = jnp.dot(w_ref[...], stacked, preferred_element_type=jnp.float32)
        out = z[0:cout, 0:STEP] + z[cout : 2 * cout, 1 : STEP + 1]
        out = out + z[2 * cout : 3 * cout, 2 : STEP + 2]
        out = out + b_ref[...]
        if extra_ref is not None:
            out = out + extra_ref[:, base : base + STEP].astype(jnp.float32)
        if relu:
            out = jnp.maximum(out, 0.0)
        out = jnp.where(keep_ref[:, base : base + STEP] > 0, out, 0.0)
        o_ref[:, base : base + STEP] = out.astype(o_ref.dtype)


def keep_lines(levels, cols, ext):
    first_level = lax.axis_index("sec") * (DISP // lax.axis_size("sec"))
    width = cols - 2 * ext
    first_col = lax.axis_index("col") * width
    total = width * lax.axis_size("col")
    level = first_level - ext + jnp.arange(DEPTH)
    col = first_col - ext + jnp.arange(LINE)
    keep_level = (level >= 0) & (level < DISP) & (jnp.arange(DEPTH) < levels)
    keep_col = (col >= 0) & (col < total) & (jnp.arange(LINE) < cols)
    return keep_level[:, None] & keep_col[None, :]


def conv_layer(planes, kernel, bias, keep, extra=None, relu=True, out_dtype=jnp.bfloat16):
    chans = planes.shape[0]
    cout, cin = kernel.shape[:2]
    rows_out = max(cout, 8)
    taps = jnp.transpose(kernel, (4, 0, 2, 3, 1))
    taps = jnp.pad(taps, ((0, 0), (0, rows_out - cout), (0, 0), (0, 0), (0, chans - cin)))
    taps = taps.reshape(3 * rows_out, 9 * chans)
    bias_col = jnp.pad(bias, (0, rows_out - cout)).reshape(rows_out, 1)
    total = 2 * DEPTH * LINE
    shifts = tuple(b * DEPTH * LINE + a * LINE for a in range(3) for b in range(3))
    assert planes.shape[1] == total + max(shifts) + 128
    operands = [planes, taps, bias_col, keep]
    if extra is not None:
        operands.append(extra)
    out = pl.pallas_call(
        functools.partial(conv_kernel, cout=rows_out, relu=relu, shifts=shifts),
        out_shape=jax.ShapeDtypeStruct((rows_out, total), out_dtype),
    )(*operands)
    return out[:cout]


def with_rows(own, levels, cols, sent):
    chans = own.shape[0]
    pad = ((0, chans - sent), (0, 0), (0, DEPTH - levels), (0, LINE - cols))
    above = jnp.pad(from_behind(own[:sent, 1:, :levels, :cols], "row", 1), pad)
    below = jnp.pad(from_behind(own[:sent, :1, :levels, :cols], "row", -1), pad)
    tail = jnp.zeros((chans, 2 * LINE + 128), own.dtype)
    parts = [above, own, below]
    return jnp.concatenate([part.reshape(chans, -1) for part in parts] + [tail], axis=1)


def shards(
    left_feat,
    right_feat,
    offsets,
    w_first,
    b_first,
    w_second,
    b_second,
    w_third,
    b_third,
    w_out,
    b_out,
):
    chans, rows, width = left_feat.shape
    levels = DISP // lax.axis_size("sec")
    count = levels + 2 * EXT
    first_level = lax.axis_index("sec") * levels
    own_shift = offsets[0, 0]
    right_ext = jnp.concatenate(
        [
            from_behind(right_feat[:, :, width - PRE :], "col", 1),
            right_feat,
            jnp.zeros((chans, rows, 2 * EXT), right_feat.dtype),
        ],
        axis=2,
    )
    start = PRE - own_shift - first_level + EXT - (count - 1)
    window = lax.dynamic_slice_in_dim(right_ext, start, width + count - 1, axis=2)
    own_corr = correlate(left_feat, window, count, width)
    corr = jnp.concatenate(
        [
            from_behind(own_corr[..., width - EXT :], "col", 1),
            own_corr,
            from_behind(own_corr[..., :EXT], "col", -1),
        ],
        axis=3,
    )
    count_cols = width + 2 * EXT
    corr = jnp.transpose(corr, (0, 2, 1, 3))
    chans_in = -(-G // 16) * 16
    corr = jnp.pad(
        corr, ((0, chans_in - G), (0, 0), (0, DEPTH - count), (0, LINE - count_cols))
    )
    corr = jnp.where(keep_lines(count, count_cols, EXT), corr, 0.0).astype(jnp.bfloat16)

    sizes = [(count - 2 * k, count_cols - 2 * k) for k in range(EXT + 1)]
    flat = 2 * DEPTH * LINE

    def keep_of(k):
        return keep_lines(sizes[k][0], sizes[k][1], EXT - k)[None].repeat(2, 0).reshape(1, flat)

    act_one = conv_layer(with_rows(corr, *sizes[0], G), w_first, b_first, keep_of(1))
    act_one = act_one.reshape(-1, 2, DEPTH, LINE)
    act_two = conv_layer(with_rows(act_one, *sizes[1], act_one.shape[0]), w_second, b_second, keep_of(2))
    act_two = act_two.reshape(-1, 2, DEPTH, LINE)
    residual = jnp.pad(act_one[:, :, 2:, 2:], ((0, 0), (0, 0), (0, 2), (0, 2))).reshape(-1, flat)
    act_three = conv_layer(
        with_rows(act_two, *sizes[2], act_two.shape[0]), w_third, b_third, keep_of(3), extra=residual
    )
    act_three = act_three.reshape(-1, 2, DEPTH, LINE)
    everywhere = jnp.ones((1, flat), jnp.float32)
    cost = conv_layer(
        with_rows(act_three, *sizes[3], act_three.shape[0]), w_out, b_out, everywhere, relu=False,
        out_dtype=jnp.float32,
    )
    cost = cost.reshape(2, DEPTH, LINE)[:, :levels, :width]
    return jnp.transpose(cost, (1, 0, 2))


def solution(mesh):
    return jax.shard_map(
        shards,
        mesh=mesh,
        in_specs=(
            P(None, "row", "col"),
            P(None, "row", "col"),
            P("row", "col"),
            P(),
            P(),
            P(),
            P(),
            P(),
            P(),
            P(),
            P(),
        ),
        out_specs=P("sec", "row", "col"),
        check_vma=False,
    )
```

```python
import functools

import jax
import jax.numpy as jnp
from jax import lax
from jax.experimental import pallas as pl
from jax.sharding import PartitionSpec as P

G = 40
DISP = 48
GS = 8
EXT = 4
PRE = 136
LINE = 384
DEPTH = 32
STEP = 1536


def from_behind(array, axis, by):
    size = lax.axis_size(axis)
    pairs = [(i, i + by) for i in range(size) if 0 <= i + by < size]
    return lax.ppermute(array, axis, pairs)


def row_halo(cells):
    above = from_behind(cells[:, :, -1:], "row", 1)
    below = from_behind(cells[:, :, :1], "row", -1)
    return jnp.concatenate([above, cells, below], axis=2)


def inside(levels, width, ext):
    first_level = lax.axis_index("sec") * (DISP // lax.axis_size("sec"))
    first_col = lax.axis_index("col") * (width - 2 * ext)
    total = (width - 2 * ext) * lax.axis_size("col")
    level = first_level - ext + jnp.arange(levels)
    col = first_col - ext + jnp.arange(width)
    keep_level = (level >= 0) & (level < DISP)
    keep_col = (col >= 0) & (col < total)
    return keep_level[:, None, None] & keep_col[None, None, :]


def conv3(volume, kernel):
    out = lax.conv_general_dilated(
        volume[None],
        kernel,
        (1, 1, 1),
        "VALID",
        dimension_numbers=("NCDHW", "OIDHW", "NCDHW"),
        preferred_element_type=jnp.float32,
    )
    return out[0]


def correlate_kernel(left_ref, window_ref, out_ref):
    rows, _, width = left_ref.shape
    count = out_ref.shape[1]
    for row in range(rows):
        left = left_ref[row].astype(jnp.float32)
        window = window_ref[row].astype(jnp.float32)
        for level in range(count):
            begin = count - 1 - level
            product = left * window[:, begin : begin + width]
            summed = product.reshape(G, GS, width).sum(axis=1)
            out_ref[row, level] = (summed / GS).astype(jnp.bfloat16)


def correlate(left, window, count, width):
    chans, rows, _ = left.shape
    out = pl.pallas_call(
        correlate_kernel,
        out_shape=jax.ShapeDtypeStruct((rows, count, G, width), jnp.bfloat16),
    )(jnp.transpose(left, (1, 0, 2)), jnp.transpose(window, (1, 0, 2)))
    return jnp.transpose(out, (2, 1, 0, 3))


def own_kernel(x_ref, w_ref, o_ref, *, cout):
    plane = DEPTH * LINE
    for row in range(2):
        weights = w_ref[row]
        for base in range(0, plane, STEP):
            stacked = jnp.concatenate(
                [
                    x_ref[:, q * plane + a * LINE + base : q * plane + a * LINE + base + STEP + 128]
                    for a in range(3)
                    for q in range(2)
                ],
                axis=0,
            )
            z = jnp.dot(weights, stacked, preferred_element_type=jnp.float32)
            out = z[0:cout, 0:STEP] + z[cout : 2 * cout, 1 : STEP + 1]
            out = out + z[2 * cout : 3 * cout, 2 : STEP + 2]
            o_ref[:, row * plane + base : row * plane + base + STEP] = out


def halo_kernel(above_ref, below_ref, w_ref, part_ref, b_ref, keep_ref, *rest, cout, relu):
    if len(rest) == 2:
        extra_ref, o_ref = rest
    else:
        extra_ref = None
        (o_ref,) = rest
    plane = DEPTH * LINE
    for row, halo_ref in ((0, above_ref), (1, below_ref)):
        weights = w_ref[row]
        for base in range(0, plane, STEP):
            stacked = jnp.concatenate(
                [halo_ref[:, a * LINE + base : a * LINE + base + STEP + 128] for a in range(3)],
                axis=0,
            )
            z = jnp.dot(weights, stacked, preferred_element_type=jnp.float32)
            out = z[0:cout, 0:STEP] + z[cout : 2 * cout, 1 : STEP + 1]
            out = out + z[2 * cout : 3 * cout, 2 : STEP + 2]
            at = row * plane + base
            out = out + part_ref[:, at : at + STEP] + b_ref[...]
            if extra_ref is not None:
                out = out + extra_ref[:, at : at + STEP].astype(jnp.float32)
            if relu:
                out = jnp.maximum(out, 0.0)
            out = jnp.where(keep_ref[:, at : at + STEP] > 0, out, 0.0)
            o_ref[:, at : at + STEP] = out.astype(o_ref.dtype)
    tail = o_ref.shape[1] - 2 * plane
    o_ref[:, 2 * plane :] = jnp.zeros((o_ref.shape[0], tail), o_ref.dtype)


def keep_lines(levels, cols, ext):
    first_level = lax.axis_index("sec") * (DISP // lax.axis_size("sec"))
    width = cols - 2 * ext
    first_col = lax.axis_index("col") * width
    total = width * lax.axis_size("col")
    level = first_level - ext + jnp.arange(DEPTH)
    col = first_col - ext + jnp.arange(LINE)
    keep_level = (level >= 0) & (level < DISP) & (jnp.arange(DEPTH) < levels)
    keep_col = (col >= 0) & (col < total) & (jnp.arange(LINE) < cols)
    return keep_level[:, None] & keep_col[None, :]


TAIL = 2 * LINE + 128


def conv_layer(own, levels, cols, sent, kernel, bias, keep, extra=None, relu=True, out_dtype=jnp.bfloat16):
    chans = own.shape[0]
    plane = DEPTH * LINE
    cout, cin = kernel.shape[:2]
    rows_out = max(cout, 8)
    taps = jnp.transpose(kernel, (3, 4, 0, 2, 1))
    taps = jnp.pad(taps, ((0, 0), (0, 0), (0, rows_out - cout), (0, 0), (0, chans - cin)))
    own_taps = jnp.stack(
        [jnp.stack([taps[q + 1 - h] for q in range(2)], axis=3) for h in range(2)]
    ).reshape(2, 3 * rows_out, 6 * chans)
    halo_taps = jnp.stack([taps[0], taps[2]]).reshape(2, 3 * rows_out, 3 * chans)
    bias_col = jnp.pad(bias, (0, rows_out - cout)).reshape(rows_out, 1)
    part = pl.pallas_call(
        functools.partial(own_kernel, cout=rows_out),
        out_shape=jax.ShapeDtypeStruct((rows_out, 2 * plane), jnp.float32),
    )(own, own_taps)
    grid4 = own[:sent, : 2 * plane].reshape(sent, 2, DEPTH, LINE)[:, :, :levels, :cols]
    pad = ((0, chans - sent), (0, DEPTH - levels), (0, LINE - cols))
    tail = jnp.zeros((chans, TAIL), own.dtype)
    above = jnp.pad(from_behind(grid4[:, 1], "row", 1), pad).reshape(chans, plane)
    below = jnp.pad(from_behind(grid4[:, 0], "row", -1), pad).reshape(chans, plane)
    above = jnp.concatenate([above, tail], axis=1)
    below = jnp.concatenate([below, tail], axis=1)
    operands = [above, below, halo_taps, part, bias_col, keep]
    if extra is not None:
        operands.append(extra)
    out = pl.pallas_call(
        functools.partial(halo_kernel, cout=rows_out, relu=relu),
        out_shape=jax.ShapeDtypeStruct((rows_out, 2 * plane + TAIL), out_dtype),
    )(*operands)
    return out[:cout]


def shards(
    left_feat,
    right_feat,
    offsets,
    w_first,
    b_first,
    w_second,
    b_second,
    w_third,
    b_third,
    w_out,
    b_out,
):
    chans, rows, width = left_feat.shape
    levels = DISP // lax.axis_size("sec")
    count = levels + 2 * EXT
    first_level = lax.axis_index("sec") * levels
    own_shift = offsets[0, 0]
    right_ext = jnp.concatenate(
        [
            from_behind(right_feat[:, :, width - PRE :], "col", 1),
            right_feat,
            jnp.zeros((chans, rows, 2 * EXT), right_feat.dtype),
        ],
        axis=2,
    )
    start = PRE - own_shift - first_level + EXT - (count - 1)
    window = lax.dynamic_slice_in_dim(right_ext, start, width + count - 1, axis=2)
    own_corr = correlate(left_feat, window, count, width)
    corr = jnp.concatenate(
        [
            from_behind(own_corr[..., width - EXT :], "col", 1),
            own_corr,
            from_behind(own_corr[..., :EXT], "col", -1),
        ],
        axis=3,
    )
    count_cols = width + 2 * EXT
    corr = jnp.transpose(corr, (0, 2, 1, 3))
    chans_in = -(-G // 16) * 16
    corr = jnp.pad(
        corr, ((0, chans_in - G), (0, 0), (0, DEPTH - count), (0, LINE - count_cols))
    )
    corr = jnp.where(keep_lines(count, count_cols, EXT), corr, 0.0).astype(jnp.bfloat16)

    sizes = [(count - 2 * k, count_cols - 2 * k) for k in range(EXT + 1)]
    flat = 2 * DEPTH * LINE

    def keep_of(k):
        return keep_lines(sizes[k][0], sizes[k][1], EXT - k)[None].repeat(2, 0).reshape(1, flat)

    own = jnp.concatenate(
        [corr.reshape(corr.shape[0], flat), jnp.zeros((corr.shape[0], TAIL), corr.dtype)], axis=1
    )
    act_one = conv_layer(own, *sizes[0], G, w_first, b_first, keep_of(1))
    act_two = conv_layer(act_one, *sizes[1], act_one.shape[0], w_second, b_second, keep_of(2))
    residual = act_one[:, :flat].reshape(-1, 2, DEPTH, LINE)[:, :, 2:, 2:]
    residual = jnp.pad(residual, ((0, 0), (0, 0), (0, 2), (0, 2))).reshape(-1, flat)
    act_three = conv_layer(
        act_two, *sizes[2], act_two.shape[0], w_third, b_third, keep_of(3), extra=residual
    )
    everywhere = jnp.ones((1, flat), jnp.float32)
    cost = conv_layer(
        act_three, *sizes[3], act_three.shape[0], w_out, b_out, everywhere, relu=False,
        out_dtype=jnp.float32,
    )
    cost = cost[0, :flat].reshape(2, DEPTH, LINE)[:, :levels, :width]
    return jnp.transpose(cost, (1, 0, 2))


def solution(mesh):
    return jax.shard_map(
        shards,
        mesh=mesh,
        in_specs=(
            P(None, "row", "col"),
            P(None, "row", "col"),
            P("row", "col"),
            P(),
            P(),
            P(),
            P(),
            P(),
            P(),
            P(),
            P(),
        ),
        out_specs=P("sec", "row", "col"),
        check_vma=False,
    )
```

```python
import functools

import jax
import jax.numpy as jnp
from jax import lax
from jax.experimental import pallas as pl
from jax.sharding import PartitionSpec as P

G = 40
DISP = 48
GS = 8
EXT = 4
PRE = 136
LINE = 384
DEPTH = 32
STEP = 1536


def from_behind(array, axis, by):
    size = lax.axis_size(axis)
    pairs = [(i, i + by) for i in range(size) if 0 <= i + by < size]
    return lax.ppermute(array, axis, pairs)


def row_halo(cells):
    above = from_behind(cells[:, :, -1:], "row", 1)
    below = from_behind(cells[:, :, :1], "row", -1)
    return jnp.concatenate([above, cells, below], axis=2)


def inside(levels, width, ext):
    first_level = lax.axis_index("sec") * (DISP // lax.axis_size("sec"))
    first_col = lax.axis_index("col") * (width - 2 * ext)
    total = (width - 2 * ext) * lax.axis_size("col")
    level = first_level - ext + jnp.arange(levels)
    col = first_col - ext + jnp.arange(width)
    keep_level = (level >= 0) & (level < DISP)
    keep_col = (col >= 0) & (col < total)
    return keep_level[:, None, None] & keep_col[None, None, :]


def conv3(volume, kernel):
    out = lax.conv_general_dilated(
        volume[None],
        kernel,
        (1, 1, 1),
        "VALID",
        dimension_numbers=("NCDHW", "OIDHW", "NCDHW"),
        preferred_element_type=jnp.float32,
    )
    return out[0]


def correlate_kernel(left_ref, window_ref, out_ref):
    rows, _, width = left_ref.shape
    count = out_ref.shape[1]
    for row in range(rows):
        left = left_ref[row].astype(jnp.float32)
        window = window_ref[row].astype(jnp.float32)
        for level in range(count):
            begin = count - 1 - level
            product = left * window[:, begin : begin + width]
            summed = product.reshape(G, GS, width).sum(axis=1)
            out_ref[row, level] = (summed / GS).astype(jnp.bfloat16)


def correlate(left, window, count, width):
    chans, rows, _ = left.shape
    out = pl.pallas_call(
        correlate_kernel,
        out_shape=jax.ShapeDtypeStruct((rows, count, G, width), jnp.bfloat16),
    )(jnp.transpose(left, (1, 0, 2)), jnp.transpose(window, (1, 0, 2)))
    return jnp.transpose(out, (2, 1, 0, 3))


def lanes(ref, start, size):
    limit = ref.shape[1]
    if start + size <= limit:
        return ref[:, start : start + size]
    rest = jnp.zeros((ref.shape[0], start + size - limit), ref.dtype)
    return jnp.concatenate([ref[:, start:limit], rest], axis=1)


def own_kernel(x_ref, w_ref, o_ref, *, cout):
    plane = DEPTH * LINE
    for row in range(2):
        weights = w_ref[row]
        for base in range(0, plane, STEP):
            stacked = jnp.concatenate(
                [
                    lanes(x_ref, q * plane + a * LINE + base, STEP + 128)
                    for a in range(3)
                    for q in range(2)
                ],
                axis=0,
            )
            z = jnp.dot(weights, stacked, preferred_element_type=jnp.float32)
            out = z[0:cout, 0:STEP] + z[cout : 2 * cout, 1 : STEP + 1]
            out = out + z[2 * cout : 3 * cout, 2 : STEP + 2]
            o_ref[:, row * plane + base : row * plane + base + STEP] = out


def halo_kernel(above_ref, below_ref, w_ref, part_ref, b_ref, keep_ref, *rest, cout, relu):
    if len(rest) == 2:
        extra_ref, o_ref = rest
    else:
        extra_ref = None
        (o_ref,) = rest
    plane = DEPTH * LINE
    for row, halo_ref in ((0, above_ref), (1, below_ref)):
        weights = w_ref[row]
        for base in range(0, plane, STEP):
            stacked = jnp.concatenate(
                [lanes(halo_ref, a * LINE + base, STEP + 128) for a in range(3)],
                axis=0,
            )
            z = jnp.dot(weights, stacked, preferred_element_type=jnp.float32)
            out = z[0:cout, 0:STEP] + z[cout : 2 * cout, 1 : STEP + 1]
            out = out + z[2 * cout : 3 * cout, 2 : STEP + 2]
            at = row * plane + base
            out = out + part_ref[:, at : at + STEP] + b_ref[...]
            if extra_ref is not None:
                out = out + extra_ref[:, at : at + STEP].astype(jnp.float32)
            if relu:
                out = jnp.maximum(out, 0.0)
            out = jnp.where(keep_ref[:, at : at + STEP] > 0, out, 0.0)
            o_ref[:, at : at + STEP] = out.astype(o_ref.dtype)


def keep_lines(levels, cols, ext):
    first_level = lax.axis_index("sec") * (DISP // lax.axis_size("sec"))
    width = cols - 2 * ext
    first_col = lax.axis_index("col") * width
    total = width * lax.axis_size("col")
    level = first_level - ext + jnp.arange(DEPTH)
    col = first_col - ext + jnp.arange(LINE)
    keep_level = (level >= 0) & (level < DISP) & (jnp.arange(DEPTH) < levels)
    keep_col = (col >= 0) & (col < total) & (jnp.arange(LINE) < cols)
    return keep_level[:, None] & keep_col[None, :]


def conv_layer(own, levels, cols, sent, kernel, bias, keep, extra=None, relu=True, out_dtype=jnp.bfloat16):
    chans = own.shape[0]
    plane = DEPTH * LINE
    cout, cin = kernel.shape[:2]
    rows_out = max(cout, 8)
    taps = jnp.transpose(kernel, (3, 4, 0, 2, 1))
    taps = jnp.pad(taps, ((0, 0), (0, 0), (0, rows_out - cout), (0, 0), (0, chans - cin)))
    own_taps = jnp.stack(
        [jnp.stack([taps[q + 1 - h] for q in range(2)], axis=3) for h in range(2)]
    ).reshape(2, 3 * rows_out, 6 * chans)
    halo_taps = jnp.stack([taps[0], taps[2]]).reshape(2, 3 * rows_out, 3 * chans)
    bias_col = jnp.pad(bias, (0, rows_out - cout)).reshape(rows_out, 1)
    part = pl.pallas_call(
        functools.partial(own_kernel, cout=rows_out),
        out_shape=jax.ShapeDtypeStruct((rows_out, 2 * plane), jnp.float32),
    )(own, own_taps)
    grid4 = own[:sent, : 2 * plane].reshape(sent, 2, DEPTH, LINE)[:, :, :levels, :cols]
    pad = ((0, chans - sent), (0, DEPTH - levels), (0, LINE - cols))
    above = jnp.pad(from_behind(grid4[:, 1], "row", 1), pad).reshape(chans, plane)
    below = jnp.pad(from_behind(grid4[:, 0], "row", -1), pad).reshape(chans, plane)
    operands = [above, below, halo_taps, part, bias_col, keep]
    if extra is not None:
        operands.append(extra)
    out = pl.pallas_call(
        functools.partial(halo_kernel, cout=rows_out, relu=relu),
        out_shape=jax.ShapeDtypeStruct((rows_out, 2 * plane), out_dtype),
    )(*operands)
    return out[:cout]


def shards(
    left_feat,
    right_feat,
    offsets,
    w_first,
    b_first,
    w_second,
    b_second,
    w_third,
    b_third,
    w_out,
    b_out,
):
    chans, rows, width = left_feat.shape
    levels = DISP // lax.axis_size("sec")
    count = levels + 2 * EXT
    first_level = lax.axis_index("sec") * levels
    own_shift = offsets[0, 0]
    right_ext = jnp.concatenate(
        [
            from_behind(right_feat[:, :, width - PRE :], "col", 1),
            right_feat,
            jnp.zeros((chans, rows, 2 * EXT), right_feat.dtype),
        ],
        axis=2,
    )
    start = PRE - own_shift - first_level + EXT - (count - 1)
    window = lax.dynamic_slice_in_dim(right_ext, start, width + count - 1, axis=2)
    own_corr = correlate(left_feat, window, count, width)
    corr = jnp.concatenate(
        [
            from_behind(own_corr[..., width - EXT :], "col", 1),
            own_corr,
            from_behind(own_corr[..., :EXT], "col", -1),
        ],
        axis=3,
    )
    count_cols = width + 2 * EXT
    corr = jnp.transpose(corr, (0, 2, 1, 3))
    chans_in = -(-G // 16) * 16
    corr = jnp.pad(
        corr, ((0, chans_in - G), (0, 0), (0, DEPTH - count), (0, LINE - count_cols))
    )
    corr = jnp.where(keep_lines(count, count_cols, EXT), corr, 0.0).astype(jnp.bfloat16)

    sizes = [(count - 2 * k, count_cols - 2 * k) for k in range(EXT + 1)]
    flat = 2 * DEPTH * LINE

    def keep_of(k):
        return keep_lines(sizes[k][0], sizes[k][1], EXT - k)[None].repeat(2, 0).reshape(1, flat)

    own = corr.reshape(corr.shape[0], flat)
    act_one = conv_layer(own, *sizes[0], G, w_first, b_first, keep_of(1))
    act_two = conv_layer(act_one, *sizes[1], act_one.shape[0], w_second, b_second, keep_of(2))
    residual = act_one[:, :flat].reshape(-1, 2, DEPTH, LINE)[:, :, 2:, 2:]
    residual = jnp.pad(residual, ((0, 0), (0, 0), (0, 2), (0, 2))).reshape(-1, flat)
    act_three = conv_layer(
        act_two, *sizes[2], act_two.shape[0], w_third, b_third, keep_of(3), extra=residual
    )
    everywhere = jnp.ones((1, flat), jnp.float32)
    cost = conv_layer(
        act_three, *sizes[3], act_three.shape[0], w_out, b_out, everywhere, relu=False,
        out_dtype=jnp.float32,
    )
    cost = cost[0, :flat].reshape(2, DEPTH, LINE)[:, :levels, :width]
    return jnp.transpose(cost, (1, 0, 2))


def solution(mesh):
    return jax.shard_map(
        shards,
        mesh=mesh,
        in_specs=(
            P(None, "row", "col"),
            P(None, "row", "col"),
            P("row", "col"),
            P(),
            P(),
            P(),
            P(),
            P(),
            P(),
            P(),
            P(),
        ),
        out_specs=P("sec", "row", "col"),
        check_vma=False,
    )
```

```python
import functools

import jax
import jax.numpy as jnp
from jax import lax
from jax.experimental import pallas as pl
from jax.sharding import PartitionSpec as P

G = 40
DISP = 48
GS = 8
EXT = 4
PRE = 136
LINE = 384
DEPTH = 32
STEP = 1536


def from_behind(array, axis, by):
    size = lax.axis_size(axis)
    pairs = [(i, i + by) for i in range(size) if 0 <= i + by < size]
    return lax.ppermute(array, axis, pairs)


def row_halo(cells):
    above = from_behind(cells[:, :, -1:], "row", 1)
    below = from_behind(cells[:, :, :1], "row", -1)
    return jnp.concatenate([above, cells, below], axis=2)


def inside(levels, width, ext):
    first_level = lax.axis_index("sec") * (DISP // lax.axis_size("sec"))
    first_col = lax.axis_index("col") * (width - 2 * ext)
    total = (width - 2 * ext) * lax.axis_size("col")
    level = first_level - ext + jnp.arange(levels)
    col = first_col - ext + jnp.arange(width)
    keep_level = (level >= 0) & (level < DISP)
    keep_col = (col >= 0) & (col < total)
    return keep_level[:, None, None] & keep_col[None, None, :]


def conv3(volume, kernel):
    out = lax.conv_general_dilated(
        volume[None],
        kernel,
        (1, 1, 1),
        "VALID",
        dimension_numbers=("NCDHW", "OIDHW", "NCDHW"),
        preferred_element_type=jnp.float32,
    )
    return out[0]


def correlate_kernel(left_ref, window_ref, out_ref):
    rows, _, _, width = left_ref.shape
    count = out_ref.shape[1]
    for row in range(rows):
        left = left_ref[row].astype(jnp.float32)
        window = window_ref[row].astype(jnp.float32)
        for level in range(count):
            begin = count - 1 - level
            product = left * window[:, :, begin : begin + width]
            summed = product.sum(axis=0)
            out_ref[row, level] = (summed / GS).astype(jnp.bfloat16)


def correlate(left, window, count, width):
    chans, rows, _ = left.shape

    def grouped(x):
        return jnp.transpose(x.reshape(G, GS, rows, x.shape[2]), (2, 1, 0, 3))

    out = pl.pallas_call(
        correlate_kernel,
        out_shape=jax.ShapeDtypeStruct((rows, count, G, width), jnp.bfloat16),
    )(grouped(left), grouped(window))
    return jnp.transpose(out, (2, 1, 0, 3))


def lanes(ref, start, size):
    limit = ref.shape[1]
    if start + size <= limit:
        return ref[:, start : start + size]
    rest = jnp.zeros((ref.shape[0], start + size - limit), ref.dtype)
    return jnp.concatenate([ref[:, start:limit], rest], axis=1)


def own_kernel(x_ref, w_ref, o_ref, *, cout):
    plane = DEPTH * LINE
    for row in range(2):
        weights = w_ref[row]
        for base in range(0, plane, STEP):
            stacked = jnp.concatenate(
                [
                    lanes(x_ref, q * plane + a * LINE + base, STEP + 128)
                    for a in range(3)
                    for q in range(2)
                ],
                axis=0,
            )
            z = jnp.dot(weights, stacked, preferred_element_type=jnp.float32)
            out = z[0:cout, 0:STEP] + z[cout : 2 * cout, 1 : STEP + 1]
            out = out + z[2 * cout : 3 * cout, 2 : STEP + 2]
            o_ref[:, row * plane + base : row * plane + base + STEP] = out


def halo_kernel(above_ref, below_ref, w_ref, part_ref, b_ref, keep_ref, *rest, cout, relu):
    if len(rest) == 2:
        extra_ref, o_ref = rest
    else:
        extra_ref = None
        (o_ref,) = rest
    plane = DEPTH * LINE
    for row, halo_ref in ((0, above_ref), (1, below_ref)):
        weights = w_ref[row]
        for base in range(0, plane, STEP):
            stacked = jnp.concatenate(
                [lanes(halo_ref, a * LINE + base, STEP + 128) for a in range(3)],
                axis=0,
            )
            z = jnp.dot(weights, stacked, preferred_element_type=jnp.float32)
            out = z[0:cout, 0:STEP] + z[cout : 2 * cout, 1 : STEP + 1]
            out = out + z[2 * cout : 3 * cout, 2 : STEP + 2]
            at = row * plane + base
            out = out + part_ref[:, at : at + STEP] + b_ref[...]
            if extra_ref is not None:
                out = out + extra_ref[:, at : at + STEP].astype(jnp.float32)
            if relu:
                out = jnp.maximum(out, 0.0)
            out = jnp.where(keep_ref[:, at : at + STEP] > 0, out, 0.0)
            o_ref[:, at : at + STEP] = out.astype(o_ref.dtype)


def keep_lines(levels, cols, ext):
    first_level = lax.axis_index("sec") * (DISP // lax.axis_size("sec"))
    width = cols - 2 * ext
    first_col = lax.axis_index("col") * width
    total = width * lax.axis_size("col")
    level = first_level - ext + jnp.arange(DEPTH)
    col = first_col - ext + jnp.arange(LINE)
    keep_level = (level >= 0) & (level < DISP) & (jnp.arange(DEPTH) < levels)
    keep_col = (col >= 0) & (col < total) & (jnp.arange(LINE) < cols)
    return keep_level[:, None] & keep_col[None, :]


def conv_layer(own, levels, cols, sent, kernel, bias, keep, extra=None, relu=True, out_dtype=jnp.bfloat16):
    chans = own.shape[0]
    plane = DEPTH * LINE
    cout, cin = kernel.shape[:2]
    rows_out = max(cout, 8)
    taps = jnp.transpose(kernel, (3, 4, 0, 2, 1))
    taps = jnp.pad(taps, ((0, 0), (0, 0), (0, rows_out - cout), (0, 0), (0, chans - cin)))
    own_taps = jnp.stack(
        [jnp.stack([taps[q + 1 - h] for q in range(2)], axis=3) for h in range(2)]
    ).reshape(2, 3 * rows_out, 6 * chans)
    halo_taps = jnp.stack([taps[0], taps[2]]).reshape(2, 3 * rows_out, 3 * chans)
    bias_col = jnp.pad(bias, (0, rows_out - cout)).reshape(rows_out, 1)
    part = pl.pallas_call(
        functools.partial(own_kernel, cout=rows_out),
        out_shape=jax.ShapeDtypeStruct((rows_out, 2 * plane), jnp.float32),
    )(own, own_taps)
    grid4 = own[:sent, : 2 * plane].reshape(sent, 2, DEPTH, LINE)[:, :, :levels, :cols]
    pad = ((0, chans - sent), (0, DEPTH - levels), (0, LINE - cols))
    above = jnp.pad(from_behind(grid4[:, 1], "row", 1), pad).reshape(chans, plane)
    below = jnp.pad(from_behind(grid4[:, 0], "row", -1), pad).reshape(chans, plane)
    operands = [above, below, halo_taps, part, bias_col, keep]
    if extra is not None:
        operands.append(extra)
    out = pl.pallas_call(
        functools.partial(halo_kernel, cout=rows_out, relu=relu),
        out_shape=jax.ShapeDtypeStruct((rows_out, 2 * plane), out_dtype),
    )(*operands)
    return out[:cout]


def shards(
    left_feat,
    right_feat,
    offsets,
    w_first,
    b_first,
    w_second,
    b_second,
    w_third,
    b_third,
    w_out,
    b_out,
):
    chans, rows, width = left_feat.shape
    levels = DISP // lax.axis_size("sec")
    count = levels + 2 * EXT
    first_level = lax.axis_index("sec") * levels
    own_shift = offsets[0, 0]
    right_ext = jnp.concatenate(
        [
            from_behind(right_feat[:, :, width - PRE :], "col", 1),
            right_feat,
            jnp.zeros((chans, rows, 2 * EXT), right_feat.dtype),
        ],
        axis=2,
    )
    start = PRE - own_shift - first_level + EXT - (count - 1)
    window = lax.dynamic_slice_in_dim(right_ext, start, width + count - 1, axis=2)
    own_corr = correlate(left_feat, window, count, width)
    corr = jnp.concatenate(
        [
            from_behind(own_corr[..., width - EXT :], "col", 1),
            own_corr,
            from_behind(own_corr[..., :EXT], "col", -1),
        ],
        axis=3,
    )
    count_cols = width + 2 * EXT
    corr = jnp.transpose(corr, (0, 2, 1, 3))
    chans_in = -(-G // 16) * 16
    corr = jnp.pad(
        corr, ((0, chans_in - G), (0, 0), (0, DEPTH - count), (0, LINE - count_cols))
    )
    corr = jnp.where(keep_lines(count, count_cols, EXT), corr, 0.0).astype(jnp.bfloat16)

    sizes = [(count - 2 * k, count_cols - 2 * k) for k in range(EXT + 1)]
    flat = 2 * DEPTH * LINE

    def keep_of(k):
        return keep_lines(sizes[k][0], sizes[k][1], EXT - k)[None].repeat(2, 0).reshape(1, flat)

    own = corr.reshape(corr.shape[0], flat)
    act_one = conv_layer(own, *sizes[0], G, w_first, b_first, keep_of(1))
    act_two = conv_layer(act_one, *sizes[1], act_one.shape[0], w_second, b_second, keep_of(2))
    residual = act_one[:, :flat].reshape(-1, 2, DEPTH, LINE)[:, :, 2:, 2:]
    residual = jnp.pad(residual, ((0, 0), (0, 0), (0, 2), (0, 2))).reshape(-1, flat)
    act_three = conv_layer(
        act_two, *sizes[2], act_two.shape[0], w_third, b_third, keep_of(3), extra=residual
    )
    everywhere = jnp.ones((1, flat), jnp.float32)
    cost = conv_layer(
        act_three, *sizes[3], act_three.shape[0], w_out, b_out, everywhere, relu=False,
        out_dtype=jnp.float32,
    )
    cost = cost[0, :flat].reshape(2, DEPTH, LINE)[:, :levels, :width]
    return jnp.transpose(cost, (1, 0, 2))


def solution(mesh):
    return jax.shard_map(
        shards,
        mesh=mesh,
        in_specs=(
            P(None, "row", "col"),
            P(None, "row", "col"),
            P("row", "col"),
            P(),
            P(),
            P(),
            P(),
            P(),
            P(),
            P(),
            P(),
        ),
        out_specs=P("sec", "row", "col"),
        check_vma=False,
    )
```

```python
import functools

import jax
import jax.numpy as jnp
from jax import lax
from jax.experimental import pallas as pl
from jax.sharding import PartitionSpec as P

G = 40
DISP = 48
GS = 8
EXT = 4
PRE = 136
LINE = 384
DEPTH = 32
STEP = 3072


def from_behind(array, axis, by):
    size = lax.axis_size(axis)
    pairs = [(i, i + by) for i in range(size) if 0 <= i + by < size]
    return lax.ppermute(array, axis, pairs)


def row_halo(cells):
    above = from_behind(cells[:, :, -1:], "row", 1)
    below = from_behind(cells[:, :, :1], "row", -1)
    return jnp.concatenate([above, cells, below], axis=2)


def inside(levels, width, ext):
    first_level = lax.axis_index("sec") * (DISP // lax.axis_size("sec"))
    first_col = lax.axis_index("col") * (width - 2 * ext)
    total = (width - 2 * ext) * lax.axis_size("col")
    level = first_level - ext + jnp.arange(levels)
    col = first_col - ext + jnp.arange(width)
    keep_level = (level >= 0) & (level < DISP)
    keep_col = (col >= 0) & (col < total)
    return keep_level[:, None, None] & keep_col[None, None, :]


def conv3(volume, kernel):
    out = lax.conv_general_dilated(
        volume[None],
        kernel,
        (1, 1, 1),
        "VALID",
        dimension_numbers=("NCDHW", "OIDHW", "NCDHW"),
        preferred_element_type=jnp.float32,
    )
    return out[0]


def correlate_kernel(left_ref, window_ref, out_ref):
    rows, _, _, width = left_ref.shape
    count = out_ref.shape[1]
    for row in range(rows):
        left = left_ref[row].astype(jnp.float32)
        window = window_ref[row].astype(jnp.float32)
        for level in range(count):
            begin = count - 1 - level
            product = left * window[:, :, begin : begin + width]
            summed = product.sum(axis=0)
            out_ref[row, level] = (summed / GS).astype(jnp.bfloat16)


def correlate(left, window, count, width):
    chans, rows, _ = left.shape

    def grouped(x):
        return jnp.transpose(x.reshape(G, GS, rows, x.shape[2]), (2, 1, 0, 3))

    out = pl.pallas_call(
        correlate_kernel,
        out_shape=jax.ShapeDtypeStruct((rows, count, G, width), jnp.bfloat16),
    )(grouped(left), grouped(window))
    return jnp.transpose(out, (2, 1, 0, 3))


def lanes(ref, start, size):
    limit = ref.shape[1]
    if start + size <= limit:
        return ref[:, start : start + size]
    rest = jnp.zeros((ref.shape[0], start + size - limit), ref.dtype)
    return jnp.concatenate([ref[:, start:limit], rest], axis=1)


def own_kernel(x_ref, w_ref, o_ref, *, cout):
    plane = DEPTH * LINE
    for row in range(2):
        weights = w_ref[row]
        for base in range(0, plane, STEP):
            stacked = jnp.concatenate(
                [
                    lanes(x_ref, q * plane + a * LINE + base, STEP + 128)
                    for a in range(3)
                    for q in range(2)
                ],
                axis=0,
            )
            z = jnp.dot(weights, stacked, preferred_element_type=jnp.float32)
            out = z[0:cout, 0:STEP] + z[cout : 2 * cout, 1 : STEP + 1]
            out = out + z[2 * cout : 3 * cout, 2 : STEP + 2]
            o_ref[:, row * plane + base : row * plane + base + STEP] = out


def halo_kernel(above_ref, below_ref, w_ref, part_ref, b_ref, keep_ref, *rest, cout, relu):
    if len(rest) == 2:
        extra_ref, o_ref = rest
    else:
        extra_ref = None
        (o_ref,) = rest
    plane = DEPTH * LINE
    for row, halo_ref in ((0, above_ref), (1, below_ref)):
        weights = w_ref[row]
        for base in range(0, plane, STEP):
            stacked = jnp.concatenate(
                [lanes(halo_ref, a * LINE + base, STEP + 128) for a in range(3)],
                axis=0,
            )
            z = jnp.dot(weights, stacked, preferred_element_type=jnp.float32)
            out = z[0:cout, 0:STEP] + z[cout : 2 * cout, 1 : STEP + 1]
            out = out + z[2 * cout : 3 * cout, 2 : STEP + 2]
            at = row * plane + base
            out = out + part_ref[:, at : at + STEP] + b_ref[...]
            if extra_ref is not None:
                out = out + extra_ref[:, at : at + STEP].astype(jnp.float32)
            if relu:
                out = jnp.maximum(out, 0.0)
            out = jnp.where(keep_ref[:, at : at + STEP] > 0, out, 0.0)
            o_ref[:, at : at + STEP] = out.astype(o_ref.dtype)


def keep_lines(levels, cols, ext):
    first_level = lax.axis_index("sec") * (DISP // lax.axis_size("sec"))
    width = cols - 2 * ext
    first_col = lax.axis_index("col") * width
    total = width * lax.axis_size("col")
    level = first_level - ext + jnp.arange(DEPTH)
    col = first_col - ext + jnp.arange(LINE)
    keep_level = (level >= 0) & (level < DISP) & (jnp.arange(DEPTH) < levels)
    keep_col = (col >= 0) & (col < total) & (jnp.arange(LINE) < cols)
    return keep_level[:, None] & keep_col[None, :]


def conv_layer(own, levels, cols, sent, kernel, bias, keep, extra=None, relu=True, out_dtype=jnp.bfloat16):
    chans = own.shape[0]
    plane = DEPTH * LINE
    cout, cin = kernel.shape[:2]
    rows_out = max(cout, 8)
    taps = jnp.transpose(kernel, (3, 4, 0, 2, 1))
    taps = jnp.pad(taps, ((0, 0), (0, 0), (0, rows_out - cout), (0, 0), (0, chans - cin)))
    own_taps = jnp.stack(
        [jnp.stack([taps[q + 1 - h] for q in range(2)], axis=3) for h in range(2)]
    ).reshape(2, 3 * rows_out, 6 * chans)
    halo_taps = jnp.stack([taps[0], taps[2]]).reshape(2, 3 * rows_out, 3 * chans)
    bias_col = jnp.pad(bias, (0, rows_out - cout)).reshape(rows_out, 1)
    part = pl.pallas_call(
        functools.partial(own_kernel, cout=rows_out),
        out_shape=jax.ShapeDtypeStruct((rows_out, 2 * plane), jnp.float32),
    )(own, own_taps)
    grid4 = own[:sent, : 2 * plane].reshape(sent, 2, DEPTH, LINE)[:, :, :levels, :cols]
    pad = ((0, chans - sent), (0, DEPTH - levels), (0, LINE - cols))
    above = jnp.pad(from_behind(grid4[:, 1], "row", 1), pad).reshape(chans, plane)
    below = jnp.pad(from_behind(grid4[:, 0], "row", -1), pad).reshape(chans, plane)
    operands = [above, below, halo_taps, part, bias_col, keep]
    if extra is not None:
        operands.append(extra)
    out = pl.pallas_call(
        functools.partial(halo_kernel, cout=rows_out, relu=relu),
        out_shape=jax.ShapeDtypeStruct((rows_out, 2 * plane), out_dtype),
    )(*operands)
    return out[:cout]


def shards(
    left_feat,
    right_feat,
    offsets,
    w_first,
    b_first,
    w_second,
    b_second,
    w_third,
    b_third,
    w_out,
    b_out,
):
    chans, rows, width = left_feat.shape
    levels = DISP // lax.axis_size("sec")
    count = levels + 2 * EXT
    first_level = lax.axis_index("sec") * levels
    own_shift = offsets[0, 0]
    right_ext = jnp.concatenate(
        [
            from_behind(right_feat[:, :, width - PRE :], "col", 1),
            right_feat,
            jnp.zeros((chans, rows, 2 * EXT), right_feat.dtype),
        ],
        axis=2,
    )
    start = PRE - own_shift - first_level + EXT - (count - 1)
    window = lax.dynamic_slice_in_dim(right_ext, start, width + count - 1, axis=2)
    own_corr = correlate(left_feat, window, count, width)
    corr = jnp.concatenate(
        [
            from_behind(own_corr[..., width - EXT :], "col", 1),
            own_corr,
            from_behind(own_corr[..., :EXT], "col", -1),
        ],
        axis=3,
    )
    count_cols = width + 2 * EXT
    corr = jnp.transpose(corr, (0, 2, 1, 3))
    chans_in = -(-G // 16) * 16
    corr = jnp.pad(
        corr, ((0, chans_in - G), (0, 0), (0, DEPTH - count), (0, LINE - count_cols))
    )
    corr = jnp.where(keep_lines(count, count_cols, EXT), corr, 0.0).astype(jnp.bfloat16)

    sizes = [(count - 2 * k, count_cols - 2 * k) for k in range(EXT + 1)]
    flat = 2 * DEPTH * LINE

    def keep_of(k):
        return keep_lines(sizes[k][0], sizes[k][1], EXT - k)[None].repeat(2, 0).reshape(1, flat)

    own = corr.reshape(corr.shape[0], flat)
    act_one = conv_layer(own, *sizes[0], G, w_first, b_first, keep_of(1))
    act_two = conv_layer(act_one, *sizes[1], act_one.shape[0], w_second, b_second, keep_of(2))
    residual = act_one[:, :flat].reshape(-1, 2, DEPTH, LINE)[:, :, 2:, 2:]
    residual = jnp.pad(residual, ((0, 0), (0, 0), (0, 2), (0, 2))).reshape(-1, flat)
    act_three = conv_layer(
        act_two, *sizes[2], act_two.shape[0], w_third, b_third, keep_of(3), extra=residual
    )
    everywhere = jnp.ones((1, flat), jnp.float32)
    cost = conv_layer(
        act_three, *sizes[3], act_three.shape[0], w_out, b_out, everywhere, relu=False,
        out_dtype=jnp.float32,
    )
    cost = cost[0, :flat].reshape(2, DEPTH, LINE)[:, :levels, :width]
    return jnp.transpose(cost, (1, 0, 2))


def solution(mesh):
    return jax.shard_map(
        shards,
        mesh=mesh,
        in_specs=(
            P(None, "row", "col"),
            P(None, "row", "col"),
            P("row", "col"),
            P(),
            P(),
            P(),
            P(),
            P(),
            P(),
            P(),
            P(),
        ),
        out_specs=P("sec", "row", "col"),
        check_vma=False,
    )
```

```python
import functools

import jax
import jax.numpy as jnp
from jax import lax
from jax.experimental import pallas as pl
from jax.sharding import PartitionSpec as P

G = 40
DISP = 48
GS = 8
EXT = 4
PRE = 136
LINE = 384
DEPTH = 32
STEP = 1536


def from_behind(array, axis, by):
    size = lax.axis_size(axis)
    pairs = [(i, i + by) for i in range(size) if 0 <= i + by < size]
    return lax.ppermute(array, axis, pairs)


def row_halo(cells):
    above = from_behind(cells[:, :, -1:], "row", 1)
    below = from_behind(cells[:, :, :1], "row", -1)
    return jnp.concatenate([above, cells, below], axis=2)


def inside(levels, width, ext):
    first_level = lax.axis_index("sec") * (DISP // lax.axis_size("sec"))
    first_col = lax.axis_index("col") * (width - 2 * ext)
    total = (width - 2 * ext) * lax.axis_size("col")
    level = first_level - ext + jnp.arange(levels)
    col = first_col - ext + jnp.arange(width)
    keep_level = (level >= 0) & (level < DISP)
    keep_col = (col >= 0) & (col < total)
    return keep_level[:, None, None] & keep_col[None, None, :]


def conv3(volume, kernel):
    out = lax.conv_general_dilated(
        volume[None],
        kernel,
        (1, 1, 1),
        "VALID",
        dimension_numbers=("NCDHW", "OIDHW", "NCDHW"),
        preferred_element_type=jnp.float32,
    )
    return out[0]


def correlate_kernel(left_ref, window_ref, out_ref):
    rows, _, _, width = left_ref.shape
    count = out_ref.shape[1]
    for row in range(rows):
        left = left_ref[row].astype(jnp.float32)
        window = window_ref[row].astype(jnp.float32)
        for level in range(count):
            begin = count - 1 - level
            product = left * window[:, :, begin : begin + width]
            summed = product.sum(axis=0)
            out_ref[row, level] = (summed / GS).astype(jnp.bfloat16)


def correlate(left, window, count, width):
    chans, rows, _ = left.shape

    def grouped(x):
        return jnp.transpose(x.reshape(G, GS, rows, x.shape[2]), (2, 1, 0, 3))

    out = pl.pallas_call(
        correlate_kernel,
        out_shape=jax.ShapeDtypeStruct((rows, count, G, width), jnp.bfloat16),
    )(grouped(left), grouped(window))
    return jnp.transpose(out, (2, 1, 0, 3))


def lanes(ref, start, size):
    limit = ref.shape[1]
    if start + size <= limit:
        return ref[:, start : start + size]
    rest = jnp.zeros((ref.shape[0], start + size - limit), ref.dtype)
    return jnp.concatenate([ref[:, start:limit], rest], axis=1)


def own_kernel(x_ref, w_ref, o_ref, *, cout):
    plane = DEPTH * LINE
    for row in range(2):
        weights = w_ref[row]
        for base in range(0, plane, STEP):
            stacked = jnp.concatenate(
                [
                    lanes(x_ref, q * plane + a * LINE + base, STEP + 128)
                    for a in range(3)
                    for q in range(2)
                ],
                axis=0,
            )
            z = jnp.dot(weights, stacked, preferred_element_type=jnp.float32)
            out = z[0:cout, 0:STEP] + z[cout : 2 * cout, 1 : STEP + 1]
            out = out + z[2 * cout : 3 * cout, 2 : STEP + 2]
            o_ref[:, row * plane + base : row * plane + base + STEP] = out


def halo_kernel(above_ref, below_ref, w_ref, part_ref, b_ref, keep_ref, *rest, cout, relu, index):
    if len(rest) == 2:
        extra_ref, o_ref = rest
    else:
        extra_ref = None
        (o_ref,) = rest
    plane = DEPTH * LINE
    for row, halo_ref in ((0, above_ref), (1, below_ref)):
        weights = w_ref[row]
        for base in range(0, plane, STEP):
            stacked = jnp.concatenate(
                [lanes(halo_ref, a * LINE + base, STEP + 128) for a in range(3)],
                axis=0,
            )
            z = jnp.dot(weights, stacked, preferred_element_type=jnp.float32)
            out = z[0:cout, 0:STEP] + z[cout : 2 * cout, 1 : STEP + 1]
            out = out + z[2 * cout : 3 * cout, 2 : STEP + 2]
            at = row * plane + base
            out = out + part_ref[:, at : at + STEP] + b_ref[index, :cout]
            if extra_ref is not None:
                out = out + extra_ref[:, at : at + STEP].astype(jnp.float32)
            if relu:
                out = jnp.maximum(out, 0.0)
            out = jnp.where(keep_ref[index : index + 1, at : at + STEP] > 0, out, 0.0)
            o_ref[:, at : at + STEP] = out.astype(o_ref.dtype)


def keep_lines(levels, cols, ext):
    first_level = lax.axis_index("sec") * (DISP // lax.axis_size("sec"))
    width = cols - 2 * ext
    first_col = lax.axis_index("col") * width
    total = width * lax.axis_size("col")
    level = first_level - ext + jnp.arange(DEPTH)
    col = first_col - ext + jnp.arange(LINE)
    keep_level = (level >= 0) & (level < DISP) & (jnp.arange(DEPTH) < levels)
    keep_col = (col >= 0) & (col < total) & (jnp.arange(LINE) < cols)
    return keep_level[:, None] & keep_col[None, :]


def conv_layer(own, levels, cols, sent, kernel, biases, keeps, index, extra=None, relu=True, out_dtype=jnp.bfloat16):
    chans = own.shape[0]
    plane = DEPTH * LINE
    cout, cin = kernel.shape[:2]
    rows_out = max(cout, 8)
    taps = jnp.transpose(kernel, (3, 4, 0, 2, 1))
    taps = jnp.pad(taps, ((0, 0), (0, 0), (0, rows_out - cout), (0, 0), (0, chans - cin)))
    own_taps = jnp.stack(
        [jnp.stack([taps[q + 1 - h] for q in range(2)], axis=3) for h in range(2)]
    ).reshape(2, 3 * rows_out, 6 * chans)
    halo_taps = jnp.stack([taps[0], taps[2]]).reshape(2, 3 * rows_out, 3 * chans)
    part = pl.pallas_call(
        functools.partial(own_kernel, cout=rows_out),
        out_shape=jax.ShapeDtypeStruct((rows_out, 2 * plane), jnp.float32),
    )(own, own_taps)
    grid4 = own[:sent, : 2 * plane].reshape(sent, 2, DEPTH, LINE)[:, :, :levels, :cols]
    pad = ((0, chans - sent), (0, DEPTH - levels), (0, LINE - cols))
    above = jnp.pad(from_behind(grid4[:, 1], "row", 1), pad).reshape(chans, plane)
    below = jnp.pad(from_behind(grid4[:, 0], "row", -1), pad).reshape(chans, plane)
    operands = [above, below, halo_taps, part, biases, keeps]
    if extra is not None:
        operands.append(extra)
    out = pl.pallas_call(
        functools.partial(halo_kernel, cout=rows_out, relu=relu, index=index),
        out_shape=jax.ShapeDtypeStruct((rows_out, 2 * plane), out_dtype),
    )(*operands)
    return out[:cout]


def shards(
    left_feat,
    right_feat,
    offsets,
    w_first,
    b_first,
    w_second,
    b_second,
    w_third,
    b_third,
    w_out,
    b_out,
):
    chans, rows, width = left_feat.shape
    levels = DISP // lax.axis_size("sec")
    count = levels + 2 * EXT
    first_level = lax.axis_index("sec") * levels
    own_shift = offsets[0, 0]
    right_ext = jnp.concatenate(
        [
            from_behind(right_feat[:, :, width - PRE :], "col", 1),
            right_feat,
            jnp.zeros((chans, rows, 2 * EXT), right_feat.dtype),
        ],
        axis=2,
    )
    start = PRE - own_shift - first_level + EXT - (count - 1)
    window = lax.dynamic_slice_in_dim(right_ext, start, width + count - 1, axis=2)
    own_corr = correlate(left_feat, window, count, width)
    corr = jnp.concatenate(
        [
            from_behind(own_corr[..., width - EXT :], "col", 1),
            own_corr,
            from_behind(own_corr[..., :EXT], "col", -1),
        ],
        axis=3,
    )
    count_cols = width + 2 * EXT
    corr = jnp.transpose(corr, (0, 2, 1, 3))
    chans_in = -(-G // 16) * 16
    corr = jnp.pad(
        corr, ((0, chans_in - G), (0, 0), (0, DEPTH - count), (0, LINE - count_cols))
    )
    corr = jnp.where(keep_lines(count, count_cols, EXT), corr, 0.0).astype(jnp.bfloat16)

    sizes = [(count - 2 * k, count_cols - 2 * k) for k in range(EXT + 1)]
    flat = 2 * DEPTH * LINE

    def keep_of(k):
        return keep_lines(sizes[k][0], sizes[k][1], EXT - k)[None].repeat(2, 0).reshape(1, flat)

    keeps = jnp.concatenate(
        [keep_of(1), keep_of(2), keep_of(3), jnp.ones((1, flat), bool)], axis=0
    ).astype(jnp.float32)
    biases = [b_first, b_second, b_third, b_out]
    rows_b = max(b.shape[0] for b in biases)
    biases = jnp.stack([jnp.pad(b, (0, rows_b - b.shape[0])) for b in biases])[:, :, None]

    own = corr.reshape(corr.shape[0], flat)
    act_one = conv_layer(own, *sizes[0], G, w_first, biases, keeps, 0)
    act_two = conv_layer(act_one, *sizes[1], act_one.shape[0], w_second, biases, keeps, 1)
    residual = act_one[:, :flat].reshape(-1, 2, DEPTH, LINE)[:, :, 2:, 2:]
    residual = jnp.pad(residual, ((0, 0), (0, 0), (0, 2), (0, 2))).reshape(-1, flat)
    act_three = conv_layer(
        act_two, *sizes[2], act_two.shape[0], w_third, biases, keeps, 2, extra=residual
    )
    cost = conv_layer(
        act_three, *sizes[3], act_three.shape[0], w_out, biases, keeps, 3, relu=False,
        out_dtype=jnp.float32,
    )
    cost = cost[0, :flat].reshape(2, DEPTH, LINE)[:, :levels, :width]
    return jnp.transpose(cost, (1, 0, 2))


def solution(mesh):
    return jax.shard_map(
        shards,
        mesh=mesh,
        in_specs=(
            P(None, "row", "col"),
            P(None, "row", "col"),
            P("row", "col"),
            P(),
            P(),
            P(),
            P(),
            P(),
            P(),
            P(),
            P(),
        ),
        out_specs=P("sec", "row", "col"),
        check_vma=False,
    )
```

```python
import functools

import jax
import jax.numpy as jnp
from jax import lax
from jax.experimental import pallas as pl
from jax.sharding import PartitionSpec as P

G = 40
DISP = 48
GS = 8
EXT = 4
PRE = 136
LINE = 384
DEPTH = 32
STEP = 1536


def from_behind(array, axis, by):
    size = lax.axis_size(axis)
    pairs = [(i, i + by) for i in range(size) if 0 <= i + by < size]
    return lax.ppermute(array, axis, pairs)


def row_halo(cells):
    above = from_behind(cells[:, :, -1:], "row", 1)
    below = from_behind(cells[:, :, :1], "row", -1)
    return jnp.concatenate([above, cells, below], axis=2)


def inside(levels, width, ext):
    first_level = lax.axis_index("sec") * (DISP // lax.axis_size("sec"))
    first_col = lax.axis_index("col") * (width - 2 * ext)
    total = (width - 2 * ext) * lax.axis_size("col")
    level = first_level - ext + jnp.arange(levels)
    col = first_col - ext + jnp.arange(width)
    keep_level = (level >= 0) & (level < DISP)
    keep_col = (col >= 0) & (col < total)
    return keep_level[:, None, None] & keep_col[None, None, :]


def conv3(volume, kernel):
    out = lax.conv_general_dilated(
        volume[None],
        kernel,
        (1, 1, 1),
        "VALID",
        dimension_numbers=("NCDHW", "OIDHW", "NCDHW"),
        preferred_element_type=jnp.float32,
    )
    return out[0]


def correlate_kernel(left_ref, window_ref, out_ref):
    rows, _, _, width = left_ref.shape
    count = out_ref.shape[1]
    for row in range(rows):
        left = left_ref[row].astype(jnp.float32)
        window = window_ref[row].astype(jnp.float32)
        for level in range(count):
            begin = count - 1 - level
            product = left * window[:, :, begin : begin + width]
            summed = product.sum(axis=0)
            out_ref[row, level] = (summed / GS).astype(jnp.bfloat16)


def correlate(left, window, count, width):
    chans, rows, _ = left.shape

    def grouped(x):
        return jnp.transpose(x.reshape(G, GS, rows, x.shape[2]), (2, 1, 0, 3))

    out = pl.pallas_call(
        correlate_kernel,
        out_shape=jax.ShapeDtypeStruct((rows, count, G, width), jnp.bfloat16),
    )(grouped(left), grouped(window))
    return jnp.transpose(out, (2, 1, 0, 3))


def lanes(ref, start, size):
    limit = ref.shape[1]
    if start + size <= limit:
        return ref[:, start : start + size]
    rest = jnp.zeros((ref.shape[0], start + size - limit), ref.dtype)
    return jnp.concatenate([ref[:, start:limit], rest], axis=1)


def own_kernel(x_ref, w_ref, o_ref, *, cout):
    plane = DEPTH * LINE
    for row in range(w_ref.shape[0]):
        weights = w_ref[row]
        for base in range(0, plane, STEP):
            stacked = jnp.concatenate(
                [
                    lanes(x_ref, q * plane + a * LINE + base, STEP + 128)
                    for a in range(3)
                    for q in range(2)
                ],
                axis=0,
            )
            z = jnp.dot(weights, stacked, preferred_element_type=jnp.float32)
            out = z[0:cout, 0:STEP] + z[cout : 2 * cout, 1 : STEP + 1]
            out = out + z[2 * cout : 3 * cout, 2 : STEP + 2]
            o_ref[:, row * plane + base : row * plane + base + STEP] = out


def halo_kernel(above_ref, below_ref, w_ref, part_ref, b_ref, keep_ref, *rest, cout, relu, index):
    if len(rest) == 2:
        extra_ref, o_ref = rest
    else:
        extra_ref = None
        (o_ref,) = rest
    plane = DEPTH * LINE
    for row, halo_ref in ((0, above_ref), (1, below_ref)):
        weights = w_ref[row]
        for base in range(0, plane, STEP):
            stacked = jnp.concatenate(
                [lanes(halo_ref, a * LINE + base, STEP + 128) for a in range(3)],
                axis=0,
            )
            z = jnp.dot(weights, stacked, preferred_element_type=jnp.float32)
            out = z[0:cout, 0:STEP] + z[cout : 2 * cout, 1 : STEP + 1]
            out = out + z[2 * cout : 3 * cout, 2 : STEP + 2]
            at = row * plane + base
            out = out + part_ref[:, at : at + STEP] + b_ref[index, :cout]
            if extra_ref is not None:
                out = out + extra_ref[:, at : at + STEP].astype(jnp.float32)
            if relu:
                out = jnp.maximum(out, 0.0)
            out = jnp.where(keep_ref[index : index + 1, at : at + STEP] > 0, out, 0.0)
            o_ref[:, at : at + STEP] = out.astype(o_ref.dtype)


def keep_lines(levels, cols, ext):
    first_level = lax.axis_index("sec") * (DISP // lax.axis_size("sec"))
    width = cols - 2 * ext
    first_col = lax.axis_index("col") * width
    total = width * lax.axis_size("col")
    level = first_level - ext + jnp.arange(DEPTH)
    col = first_col - ext + jnp.arange(LINE)
    keep_level = (level >= 0) & (level < DISP) & (jnp.arange(DEPTH) < levels)
    keep_col = (col >= 0) & (col < total) & (jnp.arange(LINE) < cols)
    return keep_level[:, None] & keep_col[None, :]


def conv_layer(own, levels, cols, sent, kernel, biases, keeps, index, extra=None, relu=True, out_dtype=jnp.bfloat16):
    chans = own.shape[0]
    plane = DEPTH * LINE
    cout, cin = kernel.shape[:2]
    rows_out = max(cout, 8)
    taps = jnp.transpose(kernel, (3, 4, 0, 2, 1))
    taps = jnp.pad(taps, ((0, 0), (0, 0), (0, rows_out - cout), (0, 0), (0, chans - cin)))
    own_taps = jnp.stack(
        [jnp.stack([taps[q + 1 - h] for q in range(2)], axis=3) for h in range(2)]
    ).reshape(2, 3 * rows_out, 6 * chans)
    halo_taps = jnp.stack([taps[0], taps[2]]).reshape(2, 3 * rows_out, 3 * chans)
    part = pl.pallas_call(
        functools.partial(own_kernel, cout=rows_out),
        out_shape=jax.ShapeDtypeStruct((rows_out, 2 * plane), jnp.float32),
    )(own, own_taps)
    grid4 = own[:sent, : 2 * plane].reshape(sent, 2, DEPTH, LINE)[:, :, :levels, :cols]
    pad = ((0, chans - sent), (0, DEPTH - levels), (0, LINE - cols))
    above = jnp.pad(from_behind(grid4[:, 1], "row", 1), pad).reshape(chans, plane)
    below = jnp.pad(from_behind(grid4[:, 0], "row", -1), pad).reshape(chans, plane)
    operands = [above, below, halo_taps, part, biases, keeps]
    if extra is not None:
        operands.append(extra)
    out = pl.pallas_call(
        functools.partial(halo_kernel, cout=rows_out, relu=relu, index=index),
        out_shape=jax.ShapeDtypeStruct((rows_out, 2 * plane), out_dtype),
    )(*operands)
    return out[:cout]


def shards(
    left_feat,
    right_feat,
    offsets,
    w_first,
    b_first,
    w_second,
    b_second,
    w_third,
    b_third,
    w_out,
    b_out,
):
    chans, rows, width = left_feat.shape
    levels = DISP // lax.axis_size("sec")
    count = levels + 2 * EXT
    first_level = lax.axis_index("sec") * levels
    own_shift = offsets[0, 0]
    right_ext = jnp.concatenate(
        [
            from_behind(right_feat[:, :, width - PRE :], "col", 1),
            right_feat,
            jnp.zeros((chans, rows, 2 * EXT), right_feat.dtype),
        ],
        axis=2,
    )
    start = PRE - own_shift - first_level + EXT - (count - 1)
    window = lax.dynamic_slice_in_dim(right_ext, start, width + count - 1, axis=2)
    own_corr = correlate(left_feat, window, count, width)
    corr = jnp.concatenate(
        [
            from_behind(own_corr[..., width - EXT :], "col", 1),
            own_corr,
            from_behind(own_corr[..., :EXT], "col", -1),
        ],
        axis=3,
    )
    count_cols = width + 2 * EXT
    corr = jnp.transpose(corr, (0, 2, 1, 3))
    chans_in = -(-G // 16) * 16
    corr = jnp.pad(
        corr, ((0, chans_in - G), (0, 0), (0, DEPTH - count), (0, LINE - count_cols))
    )
    corr = jnp.where(keep_lines(count, count_cols, EXT), corr, 0.0).astype(jnp.bfloat16)

    sizes = [(count - 2 * k, count_cols - 2 * k) for k in range(EXT + 1)]
    flat = 2 * DEPTH * LINE

    def keep_of(k):
        return keep_lines(sizes[k][0], sizes[k][1], EXT - k)[None].repeat(2, 0).reshape(1, flat)

    keeps = jnp.concatenate(
        [keep_of(1), keep_of(2), keep_of(3), jnp.ones((1, flat), bool)], axis=0
    ).astype(jnp.float32)
    biases = [b_first, b_second, b_third, b_out]
    rows_b = max(b.shape[0] for b in biases)
    biases = jnp.stack([jnp.pad(b, (0, rows_b - b.shape[0])) for b in biases])[:, :, None]

    own = corr.reshape(corr.shape[0], flat)
    act_one = conv_layer(own, *sizes[0], G, w_first, biases, keeps, 0)
    act_two = conv_layer(act_one, *sizes[1], act_one.shape[0], w_second, biases, keeps, 1)
    residual = act_one[:, :flat].reshape(-1, 2, DEPTH, LINE)[:, :, 2:, 2:]
    residual = jnp.pad(residual, ((0, 0), (0, 0), (0, 2), (0, 2))).reshape(-1, flat)
    act_three = conv_layer(
        act_two, *sizes[2], act_two.shape[0], w_third, biases, keeps, 2, extra=residual
    )
    cost = cost_head(act_three, w_out, levels, width) + b_out[0]
    return jnp.transpose(cost, (1, 0, 2))


def cost_head(own, kernel, levels, width):
    chans = own.shape[0]
    plane = DEPTH * LINE
    cout, cin = kernel.shape[:2]
    rows_out = max(cout, 8)
    taps = jnp.transpose(kernel, (3, 4, 0, 2, 1))
    taps = jnp.pad(taps, ((0, 0), (0, 0), (0, rows_out - cout), (0, 0), (0, chans - cin)))
    nothing = jnp.zeros_like(taps[0])
    slots = [
        jnp.stack([taps[q + 1 - h] if 0 <= q + 1 - h <= 2 else nothing for q in range(2)], axis=3)
        for h in (-1, 0, 1, 2)
    ]
    head_taps = jnp.stack(slots).reshape(4, 3 * rows_out, 6 * chans)
    part = pl.pallas_call(
        functools.partial(own_kernel, cout=rows_out),
        out_shape=jax.ShapeDtypeStruct((rows_out, 4 * plane), jnp.float32),
    )(own, head_taps)
    part = part[0].reshape(4, DEPTH, LINE)[:, :levels, :width]
    from_above = from_behind(part[3], "row", 1)
    from_below = from_behind(part[0], "row", -1)
    return jnp.stack([part[1] + from_above, part[2] + from_below])


def solution(mesh):
    return jax.shard_map(
        shards,
        mesh=mesh,
        in_specs=(
            P(None, "row", "col"),
            P(None, "row", "col"),
            P("row", "col"),
            P(),
            P(),
            P(),
            P(),
            P(),
            P(),
            P(),
            P(),
        ),
        out_specs=P("sec", "row", "col"),
        check_vma=False,
    )
```

```python
import functools

import jax
import jax.numpy as jnp
from jax import lax
from jax.experimental import pallas as pl
from jax.sharding import PartitionSpec as P

G = 40
DISP = 48
GS = 8
EXT = 4
PRE = 136
LINE = 384
DEPTH = 32
STEP = 1536


def from_behind(array, axis, by):
    size = lax.axis_size(axis)
    pairs = [(i, i + by) for i in range(size) if 0 <= i + by < size]
    return lax.ppermute(array, axis, pairs)


def row_halo(cells):
    above = from_behind(cells[:, :, -1:], "row", 1)
    below = from_behind(cells[:, :, :1], "row", -1)
    return jnp.concatenate([above, cells, below], axis=2)


def inside(levels, width, ext):
    first_level = lax.axis_index("sec") * (DISP // lax.axis_size("sec"))
    first_col = lax.axis_index("col") * (width - 2 * ext)
    total = (width - 2 * ext) * lax.axis_size("col")
    level = first_level - ext + jnp.arange(levels)
    col = first_col - ext + jnp.arange(width)
    keep_level = (level >= 0) & (level < DISP)
    keep_col = (col >= 0) & (col < total)
    return keep_level[:, None, None] & keep_col[None, None, :]


def conv3(volume, kernel):
    out = lax.conv_general_dilated(
        volume[None],
        kernel,
        (1, 1, 1),
        "VALID",
        dimension_numbers=("NCDHW", "OIDHW", "NCDHW"),
        preferred_element_type=jnp.float32,
    )
    return out[0]


def correlate_kernel(left_ref, window_ref, out_ref):
    rows, _, _, width = left_ref.shape
    count = out_ref.shape[1]
    for row in range(rows):
        left = left_ref[row].astype(jnp.float32)
        window = window_ref[row].astype(jnp.float32)
        for level in range(count):
            begin = count - 1 - level
            product = left * window[:, :, begin : begin + width]
            summed = product.sum(axis=0)
            out_ref[row, level] = (summed / GS).astype(jnp.bfloat16)


def correlate(left, window, count, width):
    chans, rows, _ = left.shape

    def grouped(x):
        return jnp.transpose(x.reshape(G, GS, rows, x.shape[2]), (2, 1, 0, 3))

    out = pl.pallas_call(
        correlate_kernel,
        out_shape=jax.ShapeDtypeStruct((rows, count, G, width), jnp.bfloat16),
    )(grouped(left), grouped(window))
    return jnp.transpose(out, (2, 1, 0, 3))


def lanes(ref, start, size):
    limit = ref.shape[1]
    if start + size <= limit:
        return ref[:, start : start + size]
    rest = jnp.zeros((ref.shape[0], start + size - limit), ref.dtype)
    return jnp.concatenate([ref[:, start:limit], rest], axis=1)


def own_kernel(x_ref, w_ref, o_ref, *, cout):
    plane = DEPTH * LINE
    for row in range(w_ref.shape[0]):
        weights = w_ref[row]
        for base in range(0, plane, STEP):
            stacked = jnp.concatenate(
                [
                    lanes(x_ref, q * plane + a * LINE + base, STEP + 128)
                    for a in range(3)
                    for q in range(2)
                ],
                axis=0,
            )
            z = jnp.dot(weights, stacked, preferred_element_type=jnp.float32)
            out = z[0:cout, 0:STEP] + z[cout : 2 * cout, 1 : STEP + 1]
            out = out + z[2 * cout : 3 * cout, 2 : STEP + 2]
            o_ref[:, row * plane + base : row * plane + base + STEP] = out


def halo_kernel(above_ref, below_ref, w_ref, part_ref, b_ref, keep_ref, *rest, cout, relu, index):
    if len(rest) == 2:
        extra_ref, o_ref = rest
    else:
        extra_ref = None
        (o_ref,) = rest
    plane = DEPTH * LINE
    for row, halo_ref in ((0, above_ref), (1, below_ref)):
        weights = w_ref[row]
        for base in range(0, plane, STEP):
            stacked = jnp.concatenate(
                [lanes(halo_ref, a * LINE + base, STEP + 128) for a in range(3)],
                axis=0,
            )
            z = jnp.dot(weights, stacked, preferred_element_type=jnp.float32)
            out = z[0:cout, 0:STEP] + z[cout : 2 * cout, 1 : STEP + 1]
            out = out + z[2 * cout : 3 * cout, 2 : STEP + 2]
            at = row * plane + base
            out = out + part_ref[:, at : at + STEP] + b_ref[index, :cout]
            if extra_ref is not None:
                out = out + extra_ref[:, at : at + STEP].astype(jnp.float32)
            if relu:
                out = jnp.maximum(out, 0.0)
            out = jnp.where(keep_ref[index : index + 1, at : at + STEP] > 0, out, 0.0)
            o_ref[:, at : at + STEP] = out.astype(o_ref.dtype)


def keep_lines(levels, cols, ext):
    first_level = lax.axis_index("sec") * (DISP // lax.axis_size("sec"))
    width = cols - 2 * ext
    first_col = lax.axis_index("col") * width
    total = width * lax.axis_size("col")
    level = first_level - ext + jnp.arange(DEPTH)
    col = first_col - ext + jnp.arange(LINE)
    keep_level = (level >= 0) & (level < DISP) & (jnp.arange(DEPTH) < levels)
    keep_col = (col >= 0) & (col < total) & (jnp.arange(LINE) < cols)
    return keep_level[:, None] & keep_col[None, :]


def conv_layer(own, levels, cols, sent, kernel, biases, keeps, index, extra=None, relu=True, out_dtype=jnp.bfloat16):
    chans = own.shape[0]
    plane = DEPTH * LINE
    cout, cin = kernel.shape[:2]
    rows_out = max(cout, 8)
    taps = jnp.transpose(kernel, (3, 4, 0, 2, 1))
    taps = jnp.pad(taps, ((0, 0), (0, 0), (0, rows_out - cout), (0, 0), (0, chans - cin)))
    own_taps = jnp.stack(
        [jnp.stack([taps[q + 1 - h] for q in range(2)], axis=3) for h in range(2)]
    ).reshape(2, 3 * rows_out, 6 * chans)
    halo_taps = jnp.stack([taps[0], taps[2]]).reshape(2, 3 * rows_out, 3 * chans)
    part = pl.pallas_call(
        functools.partial(own_kernel, cout=rows_out),
        out_shape=jax.ShapeDtypeStruct((rows_out, 2 * plane), jnp.float32),
    )(own, own_taps)
    grid4 = own[:sent, : 2 * plane].reshape(sent, 2, DEPTH, LINE)[:, :, :levels, :cols]
    pad = ((0, chans - sent), (0, DEPTH - levels), (0, LINE - cols))
    above = jnp.pad(from_behind(grid4[:, 1], "row", 1), pad).reshape(chans, plane)
    below = jnp.pad(from_behind(grid4[:, 0], "row", -1), pad).reshape(chans, plane)
    operands = [above, below, halo_taps, part, biases, keeps]
    if extra is not None:
        operands.append(extra)
    out = pl.pallas_call(
        functools.partial(halo_kernel, cout=rows_out, relu=relu, index=index),
        out_shape=jax.ShapeDtypeStruct((rows_out, 2 * plane), out_dtype),
    )(*operands)
    return out[:cout]


def shards(
    left_feat,
    right_feat,
    offsets,
    w_first,
    b_first,
    w_second,
    b_second,
    w_third,
    b_third,
    w_out,
    b_out,
):
    chans, rows, width = left_feat.shape
    levels = DISP // lax.axis_size("sec")
    count = levels + 2 * EXT
    first_level = lax.axis_index("sec") * levels
    own_shift = offsets[0, 0]
    right_ext = jnp.concatenate(
        [
            from_behind(right_feat[:, :, width - PRE :], "col", 1),
            right_feat,
            jnp.zeros((chans, rows, 2 * EXT), right_feat.dtype),
        ],
        axis=2,
    )
    start = PRE - own_shift - first_level + EXT - (count - 1)
    window = lax.dynamic_slice_in_dim(right_ext, start, width + count - 1, axis=2)
    own_corr = correlate(left_feat, window, count, width)
    corr = jnp.concatenate(
        [
            from_behind(own_corr[..., width - EXT :], "col", 1),
            own_corr,
            from_behind(own_corr[..., :EXT], "col", -1),
        ],
        axis=3,
    )
    count_cols = width + 2 * EXT
    corr = jnp.transpose(corr, (0, 2, 1, 3))
    chans_in = -(-G // 16) * 16
    corr = jnp.pad(
        corr, ((0, chans_in - G), (0, 0), (0, DEPTH - count), (0, LINE - count_cols))
    )
    corr = jnp.where(keep_lines(count, count_cols, EXT), corr, 0.0).astype(jnp.bfloat16)

    sizes = [(count - 2 * k, count_cols - 2 * k) for k in range(EXT + 1)]
    flat = 2 * DEPTH * LINE

    def keep_of(k):
        return keep_lines(sizes[k][0], sizes[k][1], EXT - k)[None].repeat(2, 0).reshape(1, flat)

    keeps = jnp.concatenate(
        [keep_of(1), keep_of(2), keep_of(3), jnp.ones((1, flat), bool)], axis=0
    ).astype(jnp.float32)
    biases = [b_first, b_second, b_third, b_out]
    rows_b = max(b.shape[0] for b in biases)
    biases = jnp.stack([jnp.pad(b, (0, rows_b - b.shape[0])) for b in biases])[:, :, None]

    own = corr.reshape(corr.shape[0], flat)
    act_one = conv_layer(own, *sizes[0], G, w_first, biases, keeps, 0)
    act_two = conv_layer(act_one, *sizes[1], act_one.shape[0], w_second, biases, keeps, 1)
    residual = act_one[:, :flat].reshape(-1, 2, DEPTH, LINE)[:, :, 2:, 2:]
    residual = jnp.pad(residual, ((0, 0), (0, 0), (0, 2), (0, 2))).reshape(-1, flat)
    act_three = conv_layer(
        act_two, *sizes[2], act_two.shape[0], w_third, biases, keeps, 2, extra=residual
    )
    cost = cost_head(act_three, w_out, levels, width) + b_out[0]
    return jnp.transpose(cost, (1, 0, 2))


def cost_head(own, kernel, levels, width):
    chans = own.shape[0]
    plane = DEPTH * LINE
    cout, cin = kernel.shape[:2]
    rows_out = max(cout, 8)
    taps = jnp.transpose(kernel, (3, 4, 0, 2, 1))
    taps = jnp.pad(taps, ((0, 0), (0, 0), (0, rows_out - cout), (0, 0), (0, chans - cin)))
    edges = jnp.zeros((3, rows_out, 3, 2, chans), taps.dtype)
    edges = edges.at[:, 0, :, 0].set(taps[2][:, 0]).at[:, 1, :, 1].set(taps[0][:, 0])
    slots = [edges] + [jnp.stack([taps[q + 1 - h] for q in range(2)], axis=3) for h in range(2)]
    head_taps = jnp.stack(slots).reshape(3, 3 * rows_out, 6 * chans)
    part = pl.pallas_call(
        functools.partial(own_kernel, cout=rows_out),
        out_shape=jax.ShapeDtypeStruct((rows_out, 3 * plane), jnp.float32),
    )(own, head_taps)
    part = part[:2].reshape(2, 3, DEPTH, LINE)[:, :, :levels, :width]
    from_above = from_behind(part[1, 0], "row", 1)
    from_below = from_behind(part[0, 0], "row", -1)
    return jnp.stack([part[0, 1] + from_above, part[0, 2] + from_below])


def solution(mesh):
    return jax.shard_map(
        shards,
        mesh=mesh,
        in_specs=(
            P(None, "row", "col"),
            P(None, "row", "col"),
            P("row", "col"),
            P(),
            P(),
            P(),
            P(),
            P(),
            P(),
            P(),
            P(),
        ),
        out_specs=P("sec", "row", "col"),
        check_vma=False,
    )
```

```python
import functools

import jax
import jax.numpy as jnp
from jax import lax
from jax.experimental import pallas as pl
from jax.sharding import PartitionSpec as P

G = 40
DISP = 48
GS = 8
EXT = 4
PRE = 136
LINE = 384
DEPTH = 32
STEP = 1536


def from_behind(array, axis, by):
    size = lax.axis_size(axis)
    pairs = [(i, i + by) for i in range(size) if 0 <= i + by < size]
    return lax.ppermute(array, axis, pairs)


def row_halo(cells):
    above = from_behind(cells[:, :, -1:], "row", 1)
    below = from_behind(cells[:, :, :1], "row", -1)
    return jnp.concatenate([above, cells, below], axis=2)


def inside(levels, width, ext):
    first_level = lax.axis_index("sec") * (DISP // lax.axis_size("sec"))
    first_col = lax.axis_index("col") * (width - 2 * ext)
    total = (width - 2 * ext) * lax.axis_size("col")
    level = first_level - ext + jnp.arange(levels)
    col = first_col - ext + jnp.arange(width)
    keep_level = (level >= 0) & (level < DISP)
    keep_col = (col >= 0) & (col < total)
    return keep_level[:, None, None] & keep_col[None, None, :]


def conv3(volume, kernel):
    out = lax.conv_general_dilated(
        volume[None],
        kernel,
        (1, 1, 1),
        "VALID",
        dimension_numbers=("NCDHW", "OIDHW", "NCDHW"),
        preferred_element_type=jnp.float32,
    )
    return out[0]


def correlate_kernel(left_ref, window_ref, out_ref):
    rows, _, _, width = left_ref.shape
    count = out_ref.shape[1]
    for row in range(rows):
        left = left_ref[row].astype(jnp.float32)
        window = window_ref[row].astype(jnp.float32)
        for level in range(count):
            begin = count - 1 - level
            product = left * window[:, :, begin : begin + width]
            summed = product.sum(axis=0)
            out_ref[row, level] = (summed / GS).astype(jnp.bfloat16)


def correlate(left, window, count, width):
    chans, rows, _ = left.shape

    def grouped(x):
        return jnp.transpose(x.reshape(G, GS, rows, x.shape[2]), (2, 1, 0, 3))

    out = pl.pallas_call(
        correlate_kernel,
        out_shape=jax.ShapeDtypeStruct((rows, count, G, width), jnp.bfloat16),
    )(grouped(left), grouped(window))
    return jnp.transpose(out, (2, 1, 0, 3))


def lanes(ref, start, size):
    limit = ref.shape[1]
    if start + size <= limit:
        return ref[:, start : start + size]
    rest = jnp.zeros((ref.shape[0], start + size - limit), ref.dtype)
    return jnp.concatenate([ref[:, start:limit], rest], axis=1)


def own_kernel(x_ref, w_ref, o_ref, *, cout):
    plane = DEPTH * LINE
    for row in range(w_ref.shape[0]):
        weights = w_ref[row]
        for base in range(0, plane, STEP):
            stacked = jnp.concatenate(
                [
                    lanes(x_ref, q * plane + a * LINE + base, STEP + 128)
                    for a in range(3)
                    for q in range(2)
                ],
                axis=0,
            )
            z = jnp.dot(weights, stacked, preferred_element_type=jnp.float32)
            out = z[0:cout, 0:STEP] + z[cout : 2 * cout, 1 : STEP + 1]
            out = out + z[2 * cout : 3 * cout, 2 : STEP + 2]
            o_ref[:, row * plane + base : row * plane + base + STEP] = out


def halo_kernel(above_ref, below_ref, w_ref, part_ref, b_ref, keep_ref, *rest, cout, relu, index):
    if len(rest) == 2:
        extra_ref, o_ref = rest
    else:
        extra_ref = None
        (o_ref,) = rest
    plane = DEPTH * LINE
    for row, halo_ref in ((0, above_ref), (1, below_ref)):
        weights = w_ref[row]
        for base in range(0, plane, STEP):
            stacked = jnp.concatenate(
                [lanes(halo_ref, a * LINE + base, STEP + 128) for a in range(3)],
                axis=0,
            )
            z = jnp.dot(weights, stacked, preferred_element_type=jnp.float32)
            out = z[0:cout, 0:STEP] + z[cout : 2 * cout, 1 : STEP + 1]
            out = out + z[2 * cout : 3 * cout, 2 : STEP + 2]
            at = row * plane + base
            out = out + part_ref[:, at : at + STEP] + b_ref[index, :cout]
            if extra_ref is not None:
                shifted = lanes(extra_ref, at + 2 * LINE, STEP + 128)[:, 2 : STEP + 2]
                out = out + shifted.astype(jnp.float32)
            if relu:
                out = jnp.maximum(out, 0.0)
            out = jnp.where(keep_ref[index : index + 1, at : at + STEP] > 0, out, 0.0)
            o_ref[:, at : at + STEP] = out.astype(o_ref.dtype)


def keep_lines(levels, cols, ext):
    first_level = lax.axis_index("sec") * (DISP // lax.axis_size("sec"))
    width = cols - 2 * ext
    first_col = lax.axis_index("col") * width
    total = width * lax.axis_size("col")
    level = first_level - ext + jnp.arange(DEPTH)
    col = first_col - ext + jnp.arange(LINE)
    keep_level = (level >= 0) & (level < DISP) & (jnp.arange(DEPTH) < levels)
    keep_col = (col >= 0) & (col < total) & (jnp.arange(LINE) < cols)
    return keep_level[:, None] & keep_col[None, :]


def conv_layer(own, levels, cols, sent, kernel, biases, keeps, index, extra=None, relu=True, out_dtype=jnp.bfloat16):
    chans = own.shape[0]
    plane = DEPTH * LINE
    cout, cin = kernel.shape[:2]
    rows_out = max(cout, 8)
    taps = jnp.transpose(kernel, (3, 4, 0, 2, 1))
    taps = jnp.pad(taps, ((0, 0), (0, 0), (0, rows_out - cout), (0, 0), (0, chans - cin)))
    own_taps = jnp.stack(
        [jnp.stack([taps[q + 1 - h] for q in range(2)], axis=3) for h in range(2)]
    ).reshape(2, 3 * rows_out, 6 * chans)
    halo_taps = jnp.stack([taps[0], taps[2]]).reshape(2, 3 * rows_out, 3 * chans)
    part = pl.pallas_call(
        functools.partial(own_kernel, cout=rows_out),
        out_shape=jax.ShapeDtypeStruct((rows_out, 2 * plane), jnp.float32),
    )(own, own_taps)
    grid4 = own[:sent, : 2 * plane].reshape(sent, 2, DEPTH, LINE)[:, :, :levels, :cols]
    pad = ((0, chans - sent), (0, DEPTH - levels), (0, LINE - cols))
    above = jnp.pad(from_behind(grid4[:, 1], "row", 1), pad).reshape(chans, plane)
    below = jnp.pad(from_behind(grid4[:, 0], "row", -1), pad).reshape(chans, plane)
    operands = [above, below, halo_taps, part, biases, keeps]
    if extra is not None:
        operands.append(extra)
    out = pl.pallas_call(
        functools.partial(halo_kernel, cout=rows_out, relu=relu, index=index),
        out_shape=jax.ShapeDtypeStruct((rows_out, 2 * plane), out_dtype),
    )(*operands)
    return out[:cout]


def shards(
    left_feat,
    right_feat,
    offsets,
    w_first,
    b_first,
    w_second,
    b_second,
    w_third,
    b_third,
    w_out,
    b_out,
):
    chans, rows, width = left_feat.shape
    levels = DISP // lax.axis_size("sec")
    count = levels + 2 * EXT
    first_level = lax.axis_index("sec") * levels
    own_shift = offsets[0, 0]
    right_ext = jnp.concatenate(
        [
            from_behind(right_feat[:, :, width - PRE :], "col", 1),
            right_feat,
            jnp.zeros((chans, rows, 2 * EXT), right_feat.dtype),
        ],
        axis=2,
    )
    start = PRE - own_shift - first_level + EXT - (count - 1)
    window = lax.dynamic_slice_in_dim(right_ext, start, width + count - 1, axis=2)
    own_corr = correlate(left_feat, window, count, width)
    corr = jnp.concatenate(
        [
            from_behind(own_corr[..., width - EXT :], "col", 1),
            own_corr,
            from_behind(own_corr[..., :EXT], "col", -1),
        ],
        axis=3,
    )
    count_cols = width + 2 * EXT
    corr = jnp.transpose(corr, (0, 2, 1, 3))
    chans_in = -(-G // 16) * 16
    corr = jnp.pad(
        corr, ((0, chans_in - G), (0, 0), (0, DEPTH - count), (0, LINE - count_cols))
    )
    corr = jnp.where(keep_lines(count, count_cols, EXT), corr, 0.0).astype(jnp.bfloat16)

    sizes = [(count - 2 * k, count_cols - 2 * k) for k in range(EXT + 1)]
    flat = 2 * DEPTH * LINE

    def keep_of(k):
        return keep_lines(sizes[k][0], sizes[k][1], EXT - k)[None].repeat(2, 0).reshape(1, flat)

    keeps = jnp.concatenate(
        [keep_of(1), keep_of(2), keep_of(3), jnp.ones((1, flat), bool)], axis=0
    ).astype(jnp.float32)
    biases = [b_first, b_second, b_third, b_out]
    rows_b = max(b.shape[0] for b in biases)
    biases = jnp.stack([jnp.pad(b, (0, rows_b - b.shape[0])) for b in biases])[:, :, None]

    own = corr.reshape(corr.shape[0], flat)
    act_one = conv_layer(own, *sizes[0], G, w_first, biases, keeps, 0)
    act_two = conv_layer(act_one, *sizes[1], act_one.shape[0], w_second, biases, keeps, 1)
    act_three = conv_layer(
        act_two, *sizes[2], act_two.shape[0], w_third, biases, keeps, 2, extra=act_one
    )
    cost = cost_head(act_three, w_out, levels, width) + b_out[0]
    return jnp.transpose(cost, (1, 0, 2))


def cost_head(own, kernel, levels, width):
    chans = own.shape[0]
    plane = DEPTH * LINE
    cout, cin = kernel.shape[:2]
    rows_out = max(cout, 8)
    taps = jnp.transpose(kernel, (3, 4, 0, 2, 1))
    taps = jnp.pad(taps, ((0, 0), (0, 0), (0, rows_out - cout), (0, 0), (0, chans - cin)))
    nothing = jnp.zeros_like(taps[0])
    slots = [
        jnp.stack([taps[q + 1 - h] if 0 <= q + 1 - h <= 2 else nothing for q in range(2)], axis=3)
        for h in (-1, 0, 1, 2)
    ]
    head_taps = jnp.stack(slots).reshape(4, 3 * rows_out, 6 * chans)
    part = pl.pallas_call(
        functools.partial(own_kernel, cout=rows_out),
        out_shape=jax.ShapeDtypeStruct((rows_out, 4 * plane), jnp.float32),
    )(own, head_taps)
    part = part[0].reshape(4, DEPTH, LINE)[:, :levels, :width]
    from_above = from_behind(part[3], "row", 1)
    from_below = from_behind(part[0], "row", -1)
    return jnp.stack([part[1] + from_above, part[2] + from_below])


def solution(mesh):
    return jax.shard_map(
        shards,
        mesh=mesh,
        in_specs=(
            P(None, "row", "col"),
            P(None, "row", "col"),
            P("row", "col"),
            P(),
            P(),
            P(),
            P(),
            P(),
            P(),
            P(),
            P(),
        ),
        out_specs=P("sec", "row", "col"),
        check_vma=False,
    )
```

```python
import functools

import jax
import jax.numpy as jnp
from jax import lax
from jax.experimental import pallas as pl
from jax.sharding import PartitionSpec as P

G = 40
DISP = 48
GS = 8
EXT = 4
PRE = 136
LINE = 384
DEPTH = 32
STEP = 1536


def from_behind(array, axis, by):
    size = lax.axis_size(axis)
    pairs = [(i, i + by) for i in range(size) if 0 <= i + by < size]
    return lax.ppermute(array, axis, pairs)


def row_halo(cells):
    above = from_behind(cells[:, :, -1:], "row", 1)
    below = from_behind(cells[:, :, :1], "row", -1)
    return jnp.concatenate([above, cells, below], axis=2)


def inside(levels, width, ext):
    first_level = lax.axis_index("sec") * (DISP // lax.axis_size("sec"))
    first_col = lax.axis_index("col") * (width - 2 * ext)
    total = (width - 2 * ext) * lax.axis_size("col")
    level = first_level - ext + jnp.arange(levels)
    col = first_col - ext + jnp.arange(width)
    keep_level = (level >= 0) & (level < DISP)
    keep_col = (col >= 0) & (col < total)
    return keep_level[:, None, None] & keep_col[None, None, :]


def conv3(volume, kernel):
    out = lax.conv_general_dilated(
        volume[None],
        kernel,
        (1, 1, 1),
        "VALID",
        dimension_numbers=("NCDHW", "OIDHW", "NCDHW"),
        preferred_element_type=jnp.float32,
    )
    return out[0]


def correlate_kernel(left_ref, window_ref, out_ref):
    rows, _, _, width = left_ref.shape
    count = out_ref.shape[1]
    for row in range(rows):
        left = left_ref[row].astype(jnp.float32)
        window = window_ref[row].astype(jnp.float32)
        for level in range(count):
            begin = count - 1 - level
            product = left * window[:, :, begin : begin + width]
            summed = product.sum(axis=0)
            out_ref[row, level] = (summed / GS).astype(jnp.bfloat16)


def correlate(left, window, count, width):
    chans, rows, _ = left.shape

    def grouped(x):
        return jnp.transpose(x.reshape(G, GS, rows, x.shape[2]), (2, 1, 0, 3))

    out = pl.pallas_call(
        correlate_kernel,
        out_shape=jax.ShapeDtypeStruct((rows, count, G, width), jnp.bfloat16),
    )(grouped(left), grouped(window))
    return jnp.transpose(out, (2, 1, 0, 3))


def lanes(ref, start, size):
    limit = ref.shape[1]
    if start + size <= limit:
        return ref[:, start : start + size]
    rest = jnp.zeros((ref.shape[0], start + size - limit), ref.dtype)
    return jnp.concatenate([ref[:, start:limit], rest], axis=1)


def own_kernel(x_ref, w_ref, o_ref, *, cout):
    plane = DEPTH * LINE
    for row in range(w_ref.shape[0]):
        weights = w_ref[row]
        for base in range(0, plane, STEP):
            stacked = jnp.concatenate(
                [
                    lanes(x_ref, q * plane + a * LINE + base, STEP + 128)
                    for a in range(3)
                    for q in range(2)
                ],
                axis=0,
            )
            z = jnp.dot(weights, stacked, preferred_element_type=jnp.float32)
            out = z[0:cout, 0:STEP] + z[cout : 2 * cout, 1 : STEP + 1]
            out = out + z[2 * cout : 3 * cout, 2 : STEP + 2]
            o_ref[:, row * plane + base : row * plane + base + STEP] = out


def halo_kernel(above_ref, below_ref, w_ref, part_ref, b_ref, keep_ref, *rest, cout, relu, index):
    if len(rest) == 2:
        extra_ref, o_ref = rest
    else:
        extra_ref = None
        (o_ref,) = rest
    plane = DEPTH * LINE
    for row, halo_ref in ((0, above_ref), (1, below_ref)):
        weights = w_ref[row]
        for base in range(0, plane, STEP):
            stacked = jnp.concatenate(
                [lanes(halo_ref, a * LINE + base, STEP + 128) for a in range(3)],
                axis=0,
            )
            z = jnp.dot(weights, stacked, preferred_element_type=jnp.float32)
            out = z[0:cout, 0:STEP] + z[cout : 2 * cout, 1 : STEP + 1]
            out = out + z[2 * cout : 3 * cout, 2 : STEP + 2]
            at = row * plane + base
            out = out + part_ref[:, at : at + STEP] + b_ref[index, :cout]
            if extra_ref is not None:
                shifted = lanes(extra_ref, at + 2 * LINE, STEP + 128)[:, 2 : STEP + 2]
                out = out + shifted.astype(jnp.float32)
            if relu:
                out = jnp.maximum(out, 0.0)
            out = jnp.where(keep_ref[index : index + 1, at : at + STEP] > 0, out, 0.0)
            o_ref[:, at : at + STEP] = out.astype(o_ref.dtype)


def keep_lines(levels, cols, ext):
    first_level = lax.axis_index("sec") * (DISP // lax.axis_size("sec"))
    width = cols - 2 * ext
    first_col = lax.axis_index("col") * width
    total = width * lax.axis_size("col")
    level = first_level - ext + jnp.arange(DEPTH)
    col = first_col - ext + jnp.arange(LINE)
    keep_level = (level >= 0) & (level < DISP) & (jnp.arange(DEPTH) < levels)
    keep_col = (col >= 0) & (col < total) & (jnp.arange(LINE) < cols)
    return keep_level[:, None] & keep_col[None, :]


def conv_layer(own, levels, cols, sent, kernel, biases, keeps, index, extra=None, relu=True, out_dtype=jnp.bfloat16):
    chans = own.shape[0]
    plane = DEPTH * LINE
    cout, cin = kernel.shape[:2]
    rows_out = max(cout, 8)
    taps = jnp.transpose(kernel, (3, 4, 0, 2, 1))
    taps = jnp.pad(taps, ((0, 0), (0, 0), (0, rows_out - cout), (0, 0), (0, chans - cin)))
    own_taps = jnp.stack(
        [jnp.stack([taps[q + 1 - h] for q in range(2)], axis=3) for h in range(2)]
    ).reshape(2, 3 * rows_out, 6 * chans)
    halo_taps = jnp.stack([taps[0], taps[2]]).reshape(2, 3 * rows_out, 3 * chans)
    part = pl.pallas_call(
        functools.partial(own_kernel, cout=rows_out),
        out_shape=jax.ShapeDtypeStruct((rows_out, 2 * plane), jnp.float32),
    )(own, own_taps)
    if sent == chans:
        span = levels * LINE
        pad = ((0, 0), (0, plane - span))
        above = jnp.pad(from_behind(own[:, plane : plane + span], "row", 1), pad)
        below = jnp.pad(from_behind(own[:, :span], "row", -1), pad)
    else:
        grid4 = own[:sent, : 2 * plane].reshape(sent, 2, DEPTH, LINE)[:, :, :levels, :cols]
        pad = ((0, chans - sent), (0, DEPTH - levels), (0, LINE - cols))
        above = jnp.pad(from_behind(grid4[:, 1], "row", 1), pad).reshape(chans, plane)
        below = jnp.pad(from_behind(grid4[:, 0], "row", -1), pad).reshape(chans, plane)
    operands = [above, below, halo_taps, part, biases, keeps]
    if extra is not None:
        operands.append(extra)
    out = pl.pallas_call(
        functools.partial(halo_kernel, cout=rows_out, relu=relu, index=index),
        out_shape=jax.ShapeDtypeStruct((rows_out, 2 * plane), out_dtype),
    )(*operands)
    return out[:cout]


def shards(
    left_feat,
    right_feat,
    offsets,
    w_first,
    b_first,
    w_second,
    b_second,
    w_third,
    b_third,
    w_out,
    b_out,
):
    chans, rows, width = left_feat.shape
    levels = DISP // lax.axis_size("sec")
    count = levels + 2 * EXT
    first_level = lax.axis_index("sec") * levels
    own_shift = offsets[0, 0]
    right_ext = jnp.concatenate(
        [
            from_behind(right_feat[:, :, width - PRE :], "col", 1),
            right_feat,
            jnp.zeros((chans, rows, 2 * EXT), right_feat.dtype),
        ],
        axis=2,
    )
    start = PRE - own_shift - first_level + EXT - (count - 1)
    window = lax.dynamic_slice_in_dim(right_ext, start, width + count - 1, axis=2)
    own_corr = correlate(left_feat, window, count, width)
    corr = jnp.concatenate(
        [
            from_behind(own_corr[..., width - EXT :], "col", 1),
            own_corr,
            from_behind(own_corr[..., :EXT], "col", -1),
        ],
        axis=3,
    )
    count_cols = width + 2 * EXT
    corr = jnp.transpose(corr, (0, 2, 1, 3))
    chans_in = -(-G // 16) * 16
    corr = jnp.pad(
        corr, ((0, chans_in - G), (0, 0), (0, DEPTH - count), (0, LINE - count_cols))
    )
    corr = jnp.where(keep_lines(count, count_cols, EXT), corr, 0.0).astype(jnp.bfloat16)

    sizes = [(count - 2 * k, count_cols - 2 * k) for k in range(EXT + 1)]
    flat = 2 * DEPTH * LINE

    def keep_of(k):
        return keep_lines(sizes[k][0], sizes[k][1], EXT - k)[None].repeat(2, 0).reshape(1, flat)

    keeps = jnp.concatenate(
        [keep_of(1), keep_of(2), keep_of(3), jnp.ones((1, flat), bool)], axis=0
    ).astype(jnp.float32)
    biases = [b_first, b_second, b_third, b_out]
    rows_b = max(b.shape[0] for b in biases)
    biases = jnp.stack([jnp.pad(b, (0, rows_b - b.shape[0])) for b in biases])[:, :, None]

    own = corr.reshape(corr.shape[0], flat)
    act_one = conv_layer(own, *sizes[0], G, w_first, biases, keeps, 0)
    act_two = conv_layer(act_one, *sizes[1], act_one.shape[0], w_second, biases, keeps, 1)
    act_three = conv_layer(
        act_two, *sizes[2], act_two.shape[0], w_third, biases, keeps, 2, extra=act_one
    )
    cost = cost_head(act_three, w_out, levels, width) + b_out[0]
    return jnp.transpose(cost, (1, 0, 2))


def cost_head(own, kernel, levels, width):
    chans = own.shape[0]
    plane = DEPTH * LINE
    cout, cin = kernel.shape[:2]
    rows_out = max(cout, 8)
    taps = jnp.transpose(kernel, (3, 4, 0, 2, 1))
    taps = jnp.pad(taps, ((0, 0), (0, 0), (0, rows_out - cout), (0, 0), (0, chans - cin)))
    nothing = jnp.zeros_like(taps[0])
    slots = [
        jnp.stack([taps[q + 1 - h] if 0 <= q + 1 - h <= 2 else nothing for q in range(2)], axis=3)
        for h in (-1, 0, 1, 2)
    ]
    head_taps = jnp.stack(slots).reshape(4, 3 * rows_out, 6 * chans)
    part = pl.pallas_call(
        functools.partial(own_kernel, cout=rows_out),
        out_shape=jax.ShapeDtypeStruct((rows_out, 4 * plane), jnp.float32),
    )(own, head_taps)
    part = part[0].reshape(4, DEPTH, LINE)[:, :levels, :width]
    from_above = from_behind(part[3], "row", 1)
    from_below = from_behind(part[0], "row", -1)
    return jnp.stack([part[1] + from_above, part[2] + from_below])


def solution(mesh):
    return jax.shard_map(
        shards,
        mesh=mesh,
        in_specs=(
            P(None, "row", "col"),
            P(None, "row", "col"),
            P("row", "col"),
            P(),
            P(),
            P(),
            P(),
            P(),
            P(),
            P(),
            P(),
        ),
        out_specs=P("sec", "row", "col"),
        check_vma=False,
    )
```

```python
import functools

import jax
import jax.numpy as jnp
from jax import lax
from jax.experimental import pallas as pl
from jax.sharding import PartitionSpec as P

G = 40
DISP = 48
GS = 8
EXT = 4
PRE = 136
LINE = 384
DEPTH = 32
STEP = 1536


def from_behind(array, axis, by):
    size = lax.axis_size(axis)
    pairs = [(i, i + by) for i in range(size) if 0 <= i + by < size]
    return lax.ppermute(array, axis, pairs)


def row_halo(cells):
    above = from_behind(cells[:, :, -1:], "row", 1)
    below = from_behind(cells[:, :, :1], "row", -1)
    return jnp.concatenate([above, cells, below], axis=2)


def inside(levels, width, ext):
    first_level = lax.axis_index("sec") * (DISP // lax.axis_size("sec"))
    first_col = lax.axis_index("col") * (width - 2 * ext)
    total = (width - 2 * ext) * lax.axis_size("col")
    level = first_level - ext + jnp.arange(levels)
    col = first_col - ext + jnp.arange(width)
    keep_level = (level >= 0) & (level < DISP)
    keep_col = (col >= 0) & (col < total)
    return keep_level[:, None, None] & keep_col[None, None, :]


def conv3(volume, kernel):
    out = lax.conv_general_dilated(
        volume[None],
        kernel,
        (1, 1, 1),
        "VALID",
        dimension_numbers=("NCDHW", "OIDHW", "NCDHW"),
        preferred_element_type=jnp.float32,
    )
    return out[0]


def correlate_kernel(left_ref, window_ref, out_ref):
    rows, _, _, width = left_ref.shape
    count = out_ref.shape[1]
    for row in range(rows):
        left = left_ref[row].astype(jnp.float32)
        window = window_ref[row].astype(jnp.float32)
        for level in range(count):
            begin = count - 1 - level
            product = left * window[:, :, begin : begin + width]
            summed = product.sum(axis=0)
            out_ref[row, level] = (summed / GS).astype(jnp.bfloat16)


def correlate(left, window, count, width):
    chans, rows, _ = left.shape

    def grouped(x):
        return jnp.transpose(x.reshape(G, GS, rows, x.shape[2]), (2, 1, 0, 3))

    out = pl.pallas_call(
        correlate_kernel,
        out_shape=jax.ShapeDtypeStruct((rows, count, G, width), jnp.bfloat16),
    )(grouped(left), grouped(window))
    return jnp.transpose(out, (2, 1, 0, 3))


def lanes(ref, start, size):
    limit = ref.shape[1]
    if start + size <= limit:
        return ref[:, start : start + size]
    rest = jnp.zeros((ref.shape[0], start + size - limit), ref.dtype)
    return jnp.concatenate([ref[:, start:limit], rest], axis=1)


def own_kernel(x_ref, w_ref, o_ref, *, cout):
    plane = DEPTH * LINE
    for row in range(w_ref.shape[0]):
        weights = w_ref[row]
        for base in range(0, plane, STEP):
            stacked = jnp.concatenate(
                [
                    lanes(x_ref, q * plane + a * LINE + base, STEP + 128)
                    for a in range(3)
                    for q in range(2)
                ],
                axis=0,
            )
            z = jnp.dot(weights, stacked, preferred_element_type=jnp.float32)
            out = z[0:cout, 0:STEP] + z[cout : 2 * cout, 1 : STEP + 1]
            out = out + z[2 * cout : 3 * cout, 2 : STEP + 2]
            o_ref[:, row * plane + base : row * plane + base + STEP] = out


def halo_kernel(above_ref, below_ref, w_ref, part_ref, b_ref, keep_ref, *rest, cout, relu, index):
    if len(rest) == 2:
        extra_ref, o_ref = rest
    else:
        extra_ref = None
        (o_ref,) = rest
    plane = DEPTH * LINE
    for row, halo_ref in ((0, above_ref), (1, below_ref)):
        weights = w_ref[row]
        for base in range(0, plane, STEP):
            stacked = jnp.concatenate(
                [lanes(halo_ref, a * LINE + base, STEP + 128) for a in range(3)],
                axis=0,
            )
            z = jnp.dot(weights, stacked, preferred_element_type=jnp.float32)
            out = z[0:cout, 0:STEP] + z[cout : 2 * cout, 1 : STEP + 1]
            out = out + z[2 * cout : 3 * cout, 2 : STEP + 2]
            at = row * plane + base
            out = out + part_ref[:, at : at + STEP] + b_ref[index, :cout]
            if extra_ref is not None:
                shifted = lanes(extra_ref, at + 2 * LINE, STEP + 128)[:, 2 : STEP + 2]
                out = out + shifted.astype(jnp.float32)
            if relu:
                out = jnp.maximum(out, 0.0)
            out = jnp.where(keep_ref[index : index + 1, at : at + STEP] > 0, out, 0.0)
            o_ref[:, at : at + STEP] = out.astype(o_ref.dtype)


def keep_lines(levels, cols, ext):
    first_level = lax.axis_index("sec") * (DISP // lax.axis_size("sec"))
    width = cols - 2 * ext
    first_col = lax.axis_index("col") * width
    total = width * lax.axis_size("col")
    level = first_level - ext + jnp.arange(DEPTH)
    col = first_col - ext + jnp.arange(LINE)
    keep_level = (level >= 0) & (level < DISP) & (jnp.arange(DEPTH) < levels)
    keep_col = (col >= 0) & (col < total) & (jnp.arange(LINE) < cols)
    return keep_level[:, None] & keep_col[None, :]


def conv_layer(own, levels, cols, sent, kernel, biases, keeps, index, extra=None, relu=True, out_dtype=jnp.bfloat16):
    chans = own.shape[0]
    plane = DEPTH * LINE
    cout, cin = kernel.shape[:2]
    rows_out = max(cout, 8)
    taps = jnp.transpose(kernel, (3, 4, 0, 2, 1))
    taps = jnp.pad(taps, ((0, 0), (0, 0), (0, rows_out - cout), (0, 0), (0, chans - cin)))
    own_taps = jnp.stack(
        [jnp.stack([taps[q + 1 - h] for q in range(2)], axis=3) for h in range(2)]
    ).reshape(2, 3 * rows_out, 6 * chans)
    halo_taps = jnp.stack([taps[0], taps[2]]).reshape(2, 3 * rows_out, 3 * chans)
    part = pl.pallas_call(
        functools.partial(own_kernel, cout=rows_out),
        out_shape=jax.ShapeDtypeStruct((rows_out, 2 * plane), jnp.float32),
    )(own, own_taps)
    span = levels * LINE
    pad = ((0, chans - sent), (0, plane - span))
    above = jnp.pad(from_behind(own[:sent, plane : plane + span], "row", 1), pad)
    below = jnp.pad(from_behind(own[:sent, :span], "row", -1), pad)
    operands = [above, below, halo_taps, part, biases, keeps]
    if extra is not None:
        operands.append(extra)
    out = pl.pallas_call(
        functools.partial(halo_kernel, cout=rows_out, relu=relu, index=index),
        out_shape=jax.ShapeDtypeStruct((rows_out, 2 * plane), out_dtype),
    )(*operands)
    return out[:cout]


def shards(
    left_feat,
    right_feat,
    offsets,
    w_first,
    b_first,
    w_second,
    b_second,
    w_third,
    b_third,
    w_out,
    b_out,
):
    chans, rows, width = left_feat.shape
    levels = DISP // lax.axis_size("sec")
    count = levels + 2 * EXT
    first_level = lax.axis_index("sec") * levels
    own_shift = offsets[0, 0]
    right_ext = jnp.concatenate(
        [
            from_behind(right_feat[:, :, width - PRE :], "col", 1),
            right_feat,
            jnp.zeros((chans, rows, 2 * EXT), right_feat.dtype),
        ],
        axis=2,
    )
    start = PRE - own_shift - first_level + EXT - (count - 1)
    window = lax.dynamic_slice_in_dim(right_ext, start, width + count - 1, axis=2)
    own_corr = correlate(left_feat, window, count, width)
    corr = jnp.concatenate(
        [
            from_behind(own_corr[..., width - EXT :], "col", 1),
            own_corr,
            from_behind(own_corr[..., :EXT], "col", -1),
        ],
        axis=3,
    )
    count_cols = width + 2 * EXT
    corr = jnp.transpose(corr, (0, 2, 1, 3))
    chans_in = -(-G // 16) * 16
    corr = jnp.pad(
        corr, ((0, chans_in - G), (0, 0), (0, DEPTH - count), (0, LINE - count_cols))
    )
    corr = jnp.where(keep_lines(count, count_cols, EXT), corr, 0.0).astype(jnp.bfloat16)

    sizes = [(count - 2 * k, count_cols - 2 * k) for k in range(EXT + 1)]
    flat = 2 * DEPTH * LINE

    def keep_of(k):
        return keep_lines(sizes[k][0], sizes[k][1], EXT - k)[None].repeat(2, 0).reshape(1, flat)

    keeps = jnp.concatenate(
        [keep_of(1), keep_of(2), keep_of(3), jnp.ones((1, flat), bool)], axis=0
    ).astype(jnp.float32)
    biases = [b_first, b_second, b_third, b_out]
    rows_b = max(b.shape[0] for b in biases)
    biases = jnp.stack([jnp.pad(b, (0, rows_b - b.shape[0])) for b in biases])[:, :, None]

    own = corr.reshape(corr.shape[0], flat)
    act_one = conv_layer(own, *sizes[0], G, w_first, biases, keeps, 0)
    act_two = conv_layer(act_one, *sizes[1], act_one.shape[0], w_second, biases, keeps, 1)
    act_three = conv_layer(
        act_two, *sizes[2], act_two.shape[0], w_third, biases, keeps, 2, extra=act_one
    )
    cost = cost_head(act_three, w_out, levels, width) + b_out[0]
    return jnp.transpose(cost, (1, 0, 2))


def cost_head(own, kernel, levels, width):
    chans = own.shape[0]
    plane = DEPTH * LINE
    cout, cin = kernel.shape[:2]
    rows_out = max(cout, 8)
    taps = jnp.transpose(kernel, (3, 4, 0, 2, 1))
    taps = jnp.pad(taps, ((0, 0), (0, 0), (0, rows_out - cout), (0, 0), (0, chans - cin)))
    nothing = jnp.zeros_like(taps[0])
    slots = [
        jnp.stack([taps[q + 1 - h] if 0 <= q + 1 - h <= 2 else nothing for q in range(2)], axis=3)
        for h in (-1, 0, 1, 2)
    ]
    head_taps = jnp.stack(slots).reshape(4, 3 * rows_out, 6 * chans)
    part = pl.pallas_call(
        functools.partial(own_kernel, cout=rows_out),
        out_shape=jax.ShapeDtypeStruct((rows_out, 4 * plane), jnp.float32),
    )(own, head_taps)
    part = part[0].reshape(4, DEPTH, LINE)[:, :levels, :width]
    from_above = from_behind(part[3], "row", 1)
    from_below = from_behind(part[0], "row", -1)
    return jnp.stack([part[1] + from_above, part[2] + from_below])


def solution(mesh):
    return jax.shard_map(
        shards,
        mesh=mesh,
        in_specs=(
            P(None, "row", "col"),
            P(None, "row", "col"),
            P("row", "col"),
            P(),
            P(),
            P(),
            P(),
            P(),
            P(),
            P(),
            P(),
        ),
        out_specs=P("sec", "row", "col"),
        check_vma=False,
    )
```

```python
import functools

import jax
import jax.numpy as jnp
from jax import lax
from jax.experimental import pallas as pl
from jax.sharding import PartitionSpec as P

G = 40
DISP = 48
GS = 8
EXT = 4
PRE = 136
LINE = 384
DEPTH = 32
STEP = 1536


def from_behind(array, axis, by):
    size = lax.axis_size(axis)
    pairs = [(i, i + by) for i in range(size) if 0 <= i + by < size]
    return lax.ppermute(array, axis, pairs)


def row_halo(cells):
    above = from_behind(cells[:, :, -1:], "row", 1)
    below = from_behind(cells[:, :, :1], "row", -1)
    return jnp.concatenate([above, cells, below], axis=2)


def inside(levels, width, ext):
    first_level = lax.axis_index("sec") * (DISP // lax.axis_size("sec"))
    first_col = lax.axis_index("col") * (width - 2 * ext)
    total = (width - 2 * ext) * lax.axis_size("col")
    level = first_level - ext + jnp.arange(levels)
    col = first_col - ext + jnp.arange(width)
    keep_level = (level >= 0) & (level < DISP)
    keep_col = (col >= 0) & (col < total)
    return keep_level[:, None, None] & keep_col[None, None, :]


def conv3(volume, kernel):
    out = lax.conv_general_dilated(
        volume[None],
        kernel,
        (1, 1, 1),
        "VALID",
        dimension_numbers=("NCDHW", "OIDHW", "NCDHW"),
        preferred_element_type=jnp.float32,
    )
    return out[0]


def correlate_kernel(left_ref, window_ref, out_ref):
    rows, _, _, width = left_ref.shape
    count = out_ref.shape[1]
    for row in range(rows):
        left = left_ref[row].astype(jnp.float32)
        window = window_ref[row].astype(jnp.float32)
        for level in range(count):
            begin = count - 1 - level
            product = left * window[:, :, begin : begin + width]
            summed = product.sum(axis=0)
            out_ref[row, level] = (summed / GS).astype(jnp.bfloat16)


def correlate(left, window, count, width):
    chans, rows, _ = left.shape

    def grouped(x):
        return jnp.transpose(x.reshape(G, GS, rows, x.shape[2]), (2, 1, 0, 3))

    out = pl.pallas_call(
        correlate_kernel,
        out_shape=jax.ShapeDtypeStruct((rows, count, G, width), jnp.bfloat16),
    )(grouped(left), grouped(window))
    return jnp.transpose(out, (2, 1, 0, 3))


def lanes(ref, start, size):
    limit = ref.shape[1]
    if start + size <= limit:
        return ref[:, start : start + size]
    rest = jnp.zeros((ref.shape[0], start + size - limit), ref.dtype)
    return jnp.concatenate([ref[:, start:limit], rest], axis=1)


def own_kernel(x0_ref, x1_ref, w_ref, o_ref, *, cout):
    plane = DEPTH * LINE
    for row in range(w_ref.shape[0]):
        weights = w_ref[row]
        for base in range(0, plane, STEP):
            stacked = jnp.concatenate(
                [
                    lanes(x_ref, a * LINE + base, STEP + 128)
                    for a in range(3)
                    for x_ref in (x0_ref, x1_ref)
                ],
                axis=0,
            )
            z = jnp.dot(weights, stacked, preferred_element_type=jnp.float32)
            out = z[0:cout, 0:STEP] + z[cout : 2 * cout, 1 : STEP + 1]
            out = out + z[2 * cout : 3 * cout, 2 : STEP + 2]
            o_ref[:, row * plane + base : row * plane + base + STEP] = out


def halo_kernel(halo_ref, w_ref, part_ref, b_ref, keep_ref, *rest, cout, relu, index, row):
    if len(rest) == 2:
        extra_ref, o_ref = rest
    else:
        extra_ref = None
        (o_ref,) = rest
    plane = DEPTH * LINE
    weights = w_ref[row]
    for base in range(0, plane, STEP):
        stacked = jnp.concatenate(
            [lanes(halo_ref, a * LINE + base, STEP + 128) for a in range(3)], axis=0
        )
        z = jnp.dot(weights, stacked, preferred_element_type=jnp.float32)
        out = z[0:cout, 0:STEP] + z[cout : 2 * cout, 1 : STEP + 1]
        out = out + z[2 * cout : 3 * cout, 2 : STEP + 2]
        at = row * plane + base
        out = out + part_ref[:, at : at + STEP] + b_ref[index, :cout]
        if extra_ref is not None:
            shifted = lanes(extra_ref, base + 2 * LINE, STEP + 128)[:, 2 : STEP + 2]
            out = out + shifted.astype(jnp.float32)
        if relu:
            out = jnp.maximum(out, 0.0)
        out = jnp.where(keep_ref[index : index + 1, at : at + STEP] > 0, out, 0.0)
        o_ref[:, base : base + STEP] = out.astype(o_ref.dtype)


def keep_lines(levels, cols, ext):
    first_level = lax.axis_index("sec") * (DISP // lax.axis_size("sec"))
    width = cols - 2 * ext
    first_col = lax.axis_index("col") * width
    total = width * lax.axis_size("col")
    level = first_level - ext + jnp.arange(DEPTH)
    col = first_col - ext + jnp.arange(LINE)
    keep_level = (level >= 0) & (level < DISP) & (jnp.arange(DEPTH) < levels)
    keep_col = (col >= 0) & (col < total) & (jnp.arange(LINE) < cols)
    return keep_level[:, None] & keep_col[None, :]


def conv_layer(own, levels, cols, sent, kernel, biases, keeps, index, extra=None, relu=True, out_dtype=jnp.bfloat16):
    chans = own[0].shape[0]
    plane = DEPTH * LINE
    cout, cin = kernel.shape[:2]
    rows_out = max(cout, 8)
    taps = jnp.transpose(kernel, (3, 4, 0, 2, 1))
    taps = jnp.pad(taps, ((0, 0), (0, 0), (0, rows_out - cout), (0, 0), (0, chans - cin)))
    own_taps = jnp.stack(
        [jnp.stack([taps[q + 1 - h] for q in range(2)], axis=3) for h in range(2)]
    ).reshape(2, 3 * rows_out, 6 * chans)
    halo_taps = jnp.stack([taps[0], taps[2]]).reshape(2, 3 * rows_out, 3 * chans)
    part = pl.pallas_call(
        functools.partial(own_kernel, cout=rows_out),
        out_shape=jax.ShapeDtypeStruct((rows_out, 2 * plane), jnp.float32),
    )(*own, own_taps)
    span = levels * LINE
    pad = ((0, chans - sent), (0, plane - span))
    above = jnp.pad(from_behind(own[1][:sent, :span], "row", 1), pad)
    below = jnp.pad(from_behind(own[0][:sent, :span], "row", -1), pad)
    planes = []
    for row, halo in ((0, above), (1, below)):
        operands = [halo, halo_taps, part, biases, keeps]
        if extra is not None:
            operands.append(extra[row])
        out = pl.pallas_call(
            functools.partial(halo_kernel, cout=rows_out, relu=relu, index=index, row=row),
            out_shape=jax.ShapeDtypeStruct((rows_out, plane), out_dtype),
        )(*operands)
        planes.append(out[:cout])
    return planes


def shards(
    left_feat,
    right_feat,
    offsets,
    w_first,
    b_first,
    w_second,
    b_second,
    w_third,
    b_third,
    w_out,
    b_out,
):
    chans, rows, width = left_feat.shape
    levels = DISP // lax.axis_size("sec")
    count = levels + 2 * EXT
    first_level = lax.axis_index("sec") * levels
    own_shift = offsets[0, 0]
    right_ext = jnp.concatenate(
        [
            from_behind(right_feat[:, :, width - PRE :], "col", 1),
            right_feat,
            jnp.zeros((chans, rows, 2 * EXT), right_feat.dtype),
        ],
        axis=2,
    )
    start = PRE - own_shift - first_level + EXT - (count - 1)
    window = lax.dynamic_slice_in_dim(right_ext, start, width + count - 1, axis=2)
    own_corr = correlate(left_feat, window, count, width)
    corr = jnp.concatenate(
        [
            from_behind(own_corr[..., width - EXT :], "col", 1),
            own_corr,
            from_behind(own_corr[..., :EXT], "col", -1),
        ],
        axis=3,
    )
    count_cols = width + 2 * EXT
    corr = jnp.transpose(corr, (0, 2, 1, 3))
    chans_in = -(-G // 16) * 16
    corr = jnp.pad(
        corr, ((0, chans_in - G), (0, 0), (0, DEPTH - count), (0, LINE - count_cols))
    )
    corr = jnp.where(keep_lines(count, count_cols, EXT), corr, 0.0).astype(jnp.bfloat16)

    sizes = [(count - 2 * k, count_cols - 2 * k) for k in range(EXT + 1)]
    flat = 2 * DEPTH * LINE

    def keep_of(k):
        return keep_lines(sizes[k][0], sizes[k][1], EXT - k)[None].repeat(2, 0).reshape(1, flat)

    keeps = jnp.concatenate(
        [keep_of(1), keep_of(2), keep_of(3), jnp.ones((1, flat), bool)], axis=0
    ).astype(jnp.float32)
    biases = [b_first, b_second, b_third, b_out]
    rows_b = max(b.shape[0] for b in biases)
    biases = jnp.stack([jnp.pad(b, (0, rows_b - b.shape[0])) for b in biases])[:, :, None]

    own = [corr[:, 0].reshape(corr.shape[0], flat // 2), corr[:, 1].reshape(corr.shape[0], flat // 2)]
    act_one = conv_layer(own, *sizes[0], G, w_first, biases, keeps, 0)
    act_two = conv_layer(act_one, *sizes[1], act_one[0].shape[0], w_second, biases, keeps, 1)
    act_three = conv_layer(
        act_two, *sizes[2], act_two[0].shape[0], w_third, biases, keeps, 2, extra=act_one
    )
    cost = cost_head(act_three, w_out, levels, width) + b_out[0]
    return jnp.transpose(cost, (1, 0, 2))


def cost_head(own, kernel, levels, width):
    chans = own[0].shape[0]
    plane = DEPTH * LINE
    cout, cin = kernel.shape[:2]
    rows_out = max(cout, 8)
    taps = jnp.transpose(kernel, (3, 4, 0, 2, 1))
    taps = jnp.pad(taps, ((0, 0), (0, 0), (0, rows_out - cout), (0, 0), (0, chans - cin)))
    nothing = jnp.zeros_like(taps[0])
    slots = [
        jnp.stack([taps[q + 1 - h] if 0 <= q + 1 - h <= 2 else nothing for q in range(2)], axis=3)
        for h in (-1, 0, 1, 2)
    ]
    head_taps = jnp.stack(slots).reshape(4, 3 * rows_out, 6 * chans)
    part = pl.pallas_call(
        functools.partial(own_kernel, cout=rows_out),
        out_shape=jax.ShapeDtypeStruct((rows_out, 4 * plane), jnp.float32),
    )(*own, head_taps)
    part = part[0].reshape(4, DEPTH, LINE)[:, :levels, :width]
    from_above = from_behind(part[3], "row", 1)
    from_below = from_behind(part[0], "row", -1)
    return jnp.stack([part[1] + from_above, part[2] + from_below])


def solution(mesh):
    return jax.shard_map(
        shards,
        mesh=mesh,
        in_specs=(
            P(None, "row", "col"),
            P(None, "row", "col"),
            P("row", "col"),
            P(),
            P(),
            P(),
            P(),
            P(),
            P(),
            P(),
            P(),
        ),
        out_specs=P("sec", "row", "col"),
        check_vma=False,
    )
```

```python
import functools

import jax
import jax.numpy as jnp
from jax import lax
from jax.experimental import pallas as pl
from jax.sharding import PartitionSpec as P

G = 40
DISP = 48
GS = 8
EXT = 4
PRE = 136
LINE = 384
DEPTH = 32
STEP = 1536


def from_behind(array, axis, by):
    size = lax.axis_size(axis)
    pairs = [(i, i + by) for i in range(size) if 0 <= i + by < size]
    return lax.ppermute(array, axis, pairs)


def row_halo(cells):
    above = from_behind(cells[:, :, -1:], "row", 1)
    below = from_behind(cells[:, :, :1], "row", -1)
    return jnp.concatenate([above, cells, below], axis=2)


def inside(levels, width, ext):
    first_level = lax.axis_index("sec") * (DISP // lax.axis_size("sec"))
    first_col = lax.axis_index("col") * (width - 2 * ext)
    total = (width - 2 * ext) * lax.axis_size("col")
    level = first_level - ext + jnp.arange(levels)
    col = first_col - ext + jnp.arange(width)
    keep_level = (level >= 0) & (level < DISP)
    keep_col = (col >= 0) & (col < total)
    return keep_level[:, None, None] & keep_col[None, None, :]


def conv3(volume, kernel):
    out = lax.conv_general_dilated(
        volume[None],
        kernel,
        (1, 1, 1),
        "VALID",
        dimension_numbers=("NCDHW", "OIDHW", "NCDHW"),
        preferred_element_type=jnp.float32,
    )
    return out[0]


def correlate_kernel(left_ref, window_ref, out_ref):
    rows, _, _, width = left_ref.shape
    count = out_ref.shape[1]
    for row in range(rows):
        left = left_ref[row].astype(jnp.float32)
        window = window_ref[row].astype(jnp.float32)
        for level in range(count):
            begin = count - 1 - level
            product = left * window[:, :, begin : begin + width]
            summed = product.sum(axis=0)
            out_ref[row, level] = (summed / GS).astype(jnp.bfloat16)


def correlate(left, window, count, width):
    chans, rows, _ = left.shape

    def grouped(x):
        return jnp.transpose(x.reshape(G, GS, rows, x.shape[2]), (2, 1, 0, 3))

    out = pl.pallas_call(
        correlate_kernel,
        out_shape=jax.ShapeDtypeStruct((rows, count, G, width), jnp.bfloat16),
    )(grouped(left), grouped(window))
    return jnp.transpose(out, (2, 1, 0, 3))


def lanes(ref, start, size):
    limit = ref.shape[1]
    if start + size <= limit:
        return ref[:, start : start + size]
    rest = jnp.zeros((ref.shape[0], start + size - limit), ref.dtype)
    return jnp.concatenate([ref[:, start:limit], rest], axis=1)


def own_kernel(x_ref, w_ref, o_ref, *, cout):
    plane = DEPTH * LINE
    for row in range(w_ref.shape[0]):
        weights = w_ref[row]
        for base in range(0, plane, STEP):
            stacked = jnp.concatenate(
                [
                    lanes(x_ref, q * plane + a * LINE + base, STEP + 128)
                    for a in range(3)
                    for q in range(2)
                ],
                axis=0,
            )
            z = jnp.dot(weights, stacked, preferred_element_type=jnp.float32)
            out = z[0:cout, 0:STEP] + z[cout : 2 * cout, 1 : STEP + 1]
            out = out + z[2 * cout : 3 * cout, 2 : STEP + 2]
            o_ref[:, row * plane + base : row * plane + base + STEP] = out


def halo_kernel(above_ref, below_ref, w_ref, part_ref, b_ref, keep_ref, *rest, cout, relu, index):
    if len(rest) == 2:
        extra_ref, o_ref = rest
    else:
        extra_ref = None
        (o_ref,) = rest
    plane = DEPTH * LINE
    for row, halo_ref in ((0, above_ref), (1, below_ref)):
        weights = w_ref[row]
        for base in range(0, plane, STEP):
            stacked = jnp.concatenate(
                [lanes(halo_ref, a * LINE + base, STEP + 128) for a in range(3)],
                axis=0,
            )
            z = jnp.dot(weights, stacked, preferred_element_type=jnp.float32)
            out = z[0:cout, 0:STEP] + z[cout : 2 * cout, 1 : STEP + 1]
            out = out + z[2 * cout : 3 * cout, 2 : STEP + 2]
            at = row * plane + base
            out = out + part_ref[:, at : at + STEP] + b_ref[index, :cout]
            if extra_ref is not None:
                shifted = lanes(extra_ref, at + 2 * LINE, STEP + 128)[:, 2 : STEP + 2]
                out = out + shifted.astype(jnp.float32)
            if relu:
                out = jnp.maximum(out, 0.0)
            out = jnp.where(keep_ref[index : index + 1, at : at + STEP] > 0, out, 0.0)
            o_ref[:, at : at + STEP] = out.astype(o_ref.dtype)


def keep_lines(levels, cols, ext):
    first_level = lax.axis_index("sec") * (DISP // lax.axis_size("sec"))
    width = cols - 2 * ext
    first_col = lax.axis_index("col") * width
    total = width * lax.axis_size("col")
    level = first_level - ext + jnp.arange(DEPTH)
    col = first_col - ext + jnp.arange(LINE)
    keep_level = (level >= 0) & (level < DISP) & (jnp.arange(DEPTH) < levels)
    keep_col = (col >= 0) & (col < total) & (jnp.arange(LINE) < cols)
    return keep_level[:, None] & keep_col[None, :]


def conv_layer(own, levels, cols, sent, kernel, biases, keeps, index, extra=None, relu=True, out_dtype=jnp.bfloat16):
    chans = own.shape[0]
    plane = DEPTH * LINE
    cout, cin = kernel.shape[:2]
    rows_out = max(cout, 8)
    taps = jnp.transpose(kernel, (3, 4, 0, 2, 1))
    taps = jnp.pad(taps, ((0, 0), (0, 0), (0, rows_out - cout), (0, 0), (0, chans - cin)))
    own_taps = jnp.stack(
        [jnp.stack([taps[q + 1 - h] for q in range(2)], axis=3) for h in range(2)]
    ).reshape(2, 3 * rows_out, 6 * chans)
    halo_taps = jnp.stack([taps[0], taps[2]]).reshape(2, 3 * rows_out, 3 * chans)
    part = pl.pallas_call(
        functools.partial(own_kernel, cout=rows_out),
        out_shape=jax.ShapeDtypeStruct((rows_out, 2 * plane), jnp.float32),
    )(own, own_taps)
    span = levels * LINE
    pad = ((0, chans - sent), (0, plane - span))
    above = jnp.pad(from_behind(own[:sent, plane : plane + span], "row", 1), pad)
    below = jnp.pad(from_behind(own[:sent, :span], "row", -1), pad)
    operands = [above, below, halo_taps, part, biases, keeps]
    if extra is not None:
        operands.append(extra)
    out = pl.pallas_call(
        functools.partial(halo_kernel, cout=rows_out, relu=relu, index=index),
        out_shape=jax.ShapeDtypeStruct((rows_out, 2 * plane), out_dtype),
    )(*operands)
    return out[:cout]


def shards(
    left_feat,
    right_feat,
    offsets,
    w_first,
    b_first,
    w_second,
    b_second,
    w_third,
    b_third,
    w_out,
    b_out,
):
    chans, rows, width = left_feat.shape
    levels = DISP // lax.axis_size("sec")
    count = levels + 2 * EXT
    first_level = lax.axis_index("sec") * levels
    own_shift = offsets[0, 0]
    right_ext = jnp.concatenate(
        [
            from_behind(right_feat[:, :, width - PRE :], "col", 1),
            right_feat,
            jnp.zeros((chans, rows, 2 * EXT), right_feat.dtype),
        ],
        axis=2,
    )
    start = PRE - own_shift - first_level + EXT - (count - 1)
    window = lax.dynamic_slice_in_dim(right_ext, start, width + count - 1, axis=2)
    own_corr = correlate(left_feat, window, count, width)
    corr = jnp.concatenate(
        [
            from_behind(own_corr[..., width - EXT :], "col", 1),
            own_corr,
            from_behind(own_corr[..., :EXT], "col", -1),
        ],
        axis=3,
    )
    count_cols = width + 2 * EXT
    corr = jnp.transpose(corr, (0, 2, 1, 3))
    chans_in = G
    corr = jnp.pad(
        corr, ((0, chans_in - G), (0, 0), (0, DEPTH - count), (0, LINE - count_cols))
    )
    corr = jnp.where(keep_lines(count, count_cols, EXT), corr, 0.0).astype(jnp.bfloat16)

    sizes = [(count - 2 * k, count_cols - 2 * k) for k in range(EXT + 1)]
    flat = 2 * DEPTH * LINE

    def keep_of(k):
        return keep_lines(sizes[k][0], sizes[k][1], EXT - k)[None].repeat(2, 0).reshape(1, flat)

    keeps = jnp.concatenate(
        [keep_of(1), keep_of(2), keep_of(3), jnp.ones((1, flat), bool)], axis=0
    ).astype(jnp.float32)
    biases = [b_first, b_second, b_third, b_out]
    rows_b = max(b.shape[0] for b in biases)
    biases = jnp.stack([jnp.pad(b, (0, rows_b - b.shape[0])) for b in biases])[:, :, None]

    own = corr.reshape(corr.shape[0], flat)
    act_one = conv_layer(own, *sizes[0], G, w_first, biases, keeps, 0)
    act_two = conv_layer(act_one, *sizes[1], act_one.shape[0], w_second, biases, keeps, 1)
    act_three = conv_layer(
        act_two, *sizes[2], act_two.shape[0], w_third, biases, keeps, 2, extra=act_one
    )
    cost = cost_head(act_three, w_out, levels, width) + b_out[0]
    return jnp.transpose(cost, (1, 0, 2))


def cost_head(own, kernel, levels, width):
    chans = own.shape[0]
    plane = DEPTH * LINE
    cout, cin = kernel.shape[:2]
    rows_out = max(cout, 8)
    taps = jnp.transpose(kernel, (3, 4, 0, 2, 1))
    taps = jnp.pad(taps, ((0, 0), (0, 0), (0, rows_out - cout), (0, 0), (0, chans - cin)))
    nothing = jnp.zeros_like(taps[0])
    slots = [
        jnp.stack([taps[q + 1 - h] if 0 <= q + 1 - h <= 2 else nothing for q in range(2)], axis=3)
        for h in (-1, 0, 1, 2)
    ]
    head_taps = jnp.stack(slots).reshape(4, 3 * rows_out, 6 * chans)
    part = pl.pallas_call(
        functools.partial(own_kernel, cout=rows_out),
        out_shape=jax.ShapeDtypeStruct((rows_out, 4 * plane), jnp.float32),
    )(own, head_taps)
    part = part[0].reshape(4, DEPTH, LINE)[:, :levels, :width]
    from_above = from_behind(part[3], "row", 1)
    from_below = from_behind(part[0], "row", -1)
    return jnp.stack([part[1] + from_above, part[2] + from_below])


def solution(mesh):
    return jax.shard_map(
        shards,
        mesh=mesh,
        in_specs=(
            P(None, "row", "col"),
            P(None, "row", "col"),
            P("row", "col"),
            P(),
            P(),
            P(),
            P(),
            P(),
            P(),
            P(),
            P(),
        ),
        out_specs=P("sec", "row", "col"),
        check_vma=False,
    )
```

```python
import functools

import jax
import jax.numpy as jnp
from jax import lax
from jax.experimental import pallas as pl
from jax.sharding import PartitionSpec as P

G = 40
DISP = 48
GS = 8
EXT = 4
PRE = 136
LINE = 384
DEPTH = 32
STEP = 768


def from_behind(array, axis, by):
    size = lax.axis_size(axis)
    pairs = [(i, i + by) for i in range(size) if 0 <= i + by < size]
    return lax.ppermute(array, axis, pairs)


def row_halo(cells):
    above = from_behind(cells[:, :, -1:], "row", 1)
    below = from_behind(cells[:, :, :1], "row", -1)
    return jnp.concatenate([above, cells, below], axis=2)


def inside(levels, width, ext):
    first_level = lax.axis_index("sec") * (DISP // lax.axis_size("sec"))
    first_col = lax.axis_index("col") * (width - 2 * ext)
    total = (width - 2 * ext) * lax.axis_size("col")
    level = first_level - ext + jnp.arange(levels)
    col = first_col - ext + jnp.arange(width)
    keep_level = (level >= 0) & (level < DISP)
    keep_col = (col >= 0) & (col < total)
    return keep_level[:, None, None] & keep_col[None, None, :]


def conv3(volume, kernel):
    out = lax.conv_general_dilated(
        volume[None],
        kernel,
        (1, 1, 1),
        "VALID",
        dimension_numbers=("NCDHW", "OIDHW", "NCDHW"),
        preferred_element_type=jnp.float32,
    )
    return out[0]


def correlate_kernel(left_ref, window_ref, out_ref):
    rows, _, _, width = left_ref.shape
    count = out_ref.shape[1]
    for row in range(rows):
        left = left_ref[row].astype(jnp.float32)
        window = window_ref[row].astype(jnp.float32)
        for level in range(count):
            begin = count - 1 - level
            product = left * window[:, :, begin : begin + width]
            summed = product.sum(axis=0)
            out_ref[row, level] = (summed / GS).astype(jnp.bfloat16)


def correlate(left, window, count, width):
    chans, rows, _ = left.shape

    def grouped(x):
        return jnp.transpose(x.reshape(G, GS, rows, x.shape[2]), (2, 1, 0, 3))

    out = pl.pallas_call(
        correlate_kernel,
        out_shape=jax.ShapeDtypeStruct((rows, count, G, width), jnp.bfloat16),
    )(grouped(left), grouped(window))
    return jnp.transpose(out, (2, 1, 0, 3))


def lanes(ref, start, size):
    limit = ref.shape[1]
    if start + size <= limit:
        return ref[:, start : start + size]
    if start >= limit:
        return jnp.zeros((ref.shape[0], size), ref.dtype)
    rest = jnp.zeros((ref.shape[0], start + size - limit), ref.dtype)
    return jnp.concatenate([ref[:, start:limit], rest], axis=1)


def own_kernel(x_ref, w_ref, o_ref, *, cout):
    plane = DEPTH * LINE
    for row in range(w_ref.shape[0]):
        weights = w_ref[row]
        for base in range(0, plane, STEP):
            stacked = jnp.concatenate(
                [
                    lanes(x_ref, q * plane + a * LINE + base, STEP + 128)
                    for a in range(3)
                    for q in range(2)
                ],
                axis=0,
            )
            z = jnp.dot(weights, stacked, preferred_element_type=jnp.float32)
            out = z[0:cout, 0:STEP] + z[cout : 2 * cout, 1 : STEP + 1]
            out = out + z[2 * cout : 3 * cout, 2 : STEP + 2]
            o_ref[:, row * plane + base : row * plane + base + STEP] = out


def halo_kernel(above_ref, below_ref, w_ref, part_ref, b_ref, keep_ref, *rest, cout, relu, index):
    if len(rest) == 2:
        extra_ref, o_ref = rest
    else:
        extra_ref = None
        (o_ref,) = rest
    plane = DEPTH * LINE
    for row, halo_ref in ((0, above_ref), (1, below_ref)):
        weights = w_ref[row]
        for base in range(0, plane, STEP):
            stacked = jnp.concatenate(
                [lanes(halo_ref, a * LINE + base, STEP + 128) for a in range(3)],
                axis=0,
            )
            z = jnp.dot(weights, stacked, preferred_element_type=jnp.float32)
            out = z[0:cout, 0:STEP] + z[cout : 2 * cout, 1 : STEP + 1]
            out = out + z[2 * cout : 3 * cout, 2 : STEP + 2]
            at = row * plane + base
            out = out + part_ref[:, at : at + STEP] + b_ref[index, :cout]
            if extra_ref is not None:
                shifted = lanes(extra_ref, at + 2 * LINE, STEP + 128)[:, 2 : STEP + 2]
                out = out + shifted.astype(jnp.float32)
            if relu:
                out = jnp.maximum(out, 0.0)
            out = jnp.where(keep_ref[index : index + 1, at : at + STEP] > 0, out, 0.0)
            o_ref[:, at : at + STEP] = out.astype(o_ref.dtype)


def keep_lines(levels, cols, ext):
    first_level = lax.axis_index("sec") * (DISP // lax.axis_size("sec"))
    width = cols - 2 * ext
    first_col = lax.axis_index("col") * width
    total = width * lax.axis_size("col")
    level = first_level - ext + jnp.arange(DEPTH)
    col = first_col - ext + jnp.arange(LINE)
    keep_level = (level >= 0) & (level < DISP) & (jnp.arange(DEPTH) < levels)
    keep_col = (col >= 0) & (col < total) & (jnp.arange(LINE) < cols)
    return keep_level[:, None] & keep_col[None, :]


def conv_layer(own, levels, cols, sent, kernel, biases, keeps, index, extra=None, relu=True, out_dtype=jnp.bfloat16):
    chans = own.shape[0]
    plane = DEPTH * LINE
    cout, cin = kernel.shape[:2]
    rows_out = max(cout, 8)
    taps = jnp.transpose(kernel, (3, 4, 0, 2, 1))
    taps = jnp.pad(taps, ((0, 0), (0, 0), (0, rows_out - cout), (0, 0), (0, chans - cin)))
    own_taps = jnp.stack(
        [jnp.stack([taps[q + 1 - h] for q in range(2)], axis=3) for h in range(2)]
    ).reshape(2, 3 * rows_out, 6 * chans)
    halo_taps = jnp.stack([taps[0], taps[2]]).reshape(2, 3 * rows_out, 3 * chans)
    part = pl.pallas_call(
        functools.partial(own_kernel, cout=rows_out),
        out_shape=jax.ShapeDtypeStruct((rows_out, 2 * plane), jnp.float32),
    )(own, own_taps)
    span = levels * LINE
    pad = ((0, chans - sent), (0, plane - span))
    above = jnp.pad(from_behind(own[:sent, plane : plane + span], "row", 1), pad)
    below = jnp.pad(from_behind(own[:sent, :span], "row", -1), pad)
    operands = [above, below, halo_taps, part, biases, keeps]
    if extra is not None:
        operands.append(extra)
    out = pl.pallas_call(
        functools.partial(halo_kernel, cout=rows_out, relu=relu, index=index),
        out_shape=jax.ShapeDtypeStruct((rows_out, 2 * plane), out_dtype),
    )(*operands)
    return out[:cout]


def shards(
    left_feat,
    right_feat,
    offsets,
    w_first,
    b_first,
    w_second,
    b_second,
    w_third,
    b_third,
    w_out,
    b_out,
):
    chans, rows, width = left_feat.shape
    levels = DISP // lax.axis_size("sec")
    count = levels + 2 * EXT
    first_level = lax.axis_index("sec") * levels
    own_shift = offsets[0, 0]
    right_ext = jnp.concatenate(
        [
            from_behind(right_feat[:, :, width - PRE :], "col", 1),
            right_feat,
            jnp.zeros((chans, rows, 2 * EXT), right_feat.dtype),
        ],
        axis=2,
    )
    start = PRE - own_shift - first_level + EXT - (count - 1)
    window = lax.dynamic_slice_in_dim(right_ext, start, width + count - 1, axis=2)
    own_corr = correlate(left_feat, window, count, width)
    corr = jnp.concatenate(
        [
            from_behind(own_corr[..., width - EXT :], "col", 1),
            own_corr,
            from_behind(own_corr[..., :EXT], "col", -1),
        ],
        axis=3,
    )
    count_cols = width + 2 * EXT
    corr = jnp.transpose(corr, (0, 2, 1, 3))
    chans_in = G
    corr = jnp.pad(
        corr, ((0, chans_in - G), (0, 0), (0, DEPTH - count), (0, LINE - count_cols))
    )
    corr = jnp.where(keep_lines(count, count_cols, EXT), corr, 0.0).astype(jnp.bfloat16)

    sizes = [(count - 2 * k, count_cols - 2 * k) for k in range(EXT + 1)]
    flat = 2 * DEPTH * LINE

    def keep_of(k):
        return keep_lines(sizes[k][0], sizes[k][1], EXT - k)[None].repeat(2, 0).reshape(1, flat)

    keeps = jnp.concatenate(
        [keep_of(1), keep_of(2), keep_of(3), jnp.ones((1, flat), bool)], axis=0
    ).astype(jnp.float32)
    biases = [b_first, b_second, b_third, b_out]
    rows_b = max(b.shape[0] for b in biases)
    biases = jnp.stack([jnp.pad(b, (0, rows_b - b.shape[0])) for b in biases])[:, :, None]

    own = corr.reshape(corr.shape[0], flat)
    act_one = conv_layer(own, *sizes[0], G, w_first, biases, keeps, 0)
    act_two = conv_layer(act_one, *sizes[1], act_one.shape[0], w_second, biases, keeps, 1)
    act_three = conv_layer(
        act_two, *sizes[2], act_two.shape[0], w_third, biases, keeps, 2, extra=act_one
    )
    cost = cost_head(act_three, w_out, levels, width) + b_out[0]
    return jnp.transpose(cost, (1, 0, 2))


def cost_head(own, kernel, levels, width):
    chans = own.shape[0]
    plane = DEPTH * LINE
    cout, cin = kernel.shape[:2]
    rows_out = max(cout, 8)
    taps = jnp.transpose(kernel, (3, 4, 0, 2, 1))
    taps = jnp.pad(taps, ((0, 0), (0, 0), (0, rows_out - cout), (0, 0), (0, chans - cin)))
    nothing = jnp.zeros_like(taps[0])
    slots = [
        jnp.stack([taps[q + 1 - h] if 0 <= q + 1 - h <= 2 else nothing for q in range(2)], axis=3)
        for h in (-1, 0, 1, 2)
    ]
    head_taps = jnp.stack(slots).reshape(4, 3 * rows_out, 6 * chans)
    part = pl.pallas_call(
        functools.partial(own_kernel, cout=rows_out),
        out_shape=jax.ShapeDtypeStruct((rows_out, 4 * plane), jnp.float32),
    )(own, head_taps)
    part = part[0].reshape(4, DEPTH, LINE)[:, :levels, :width]
    from_above = from_behind(part[3], "row", 1)
    from_below = from_behind(part[0], "row", -1)
    return jnp.stack([part[1] + from_above, part[2] + from_below])


def solution(mesh):
    return jax.shard_map(
        shards,
        mesh=mesh,
        in_specs=(
            P(None, "row", "col"),
            P(None, "row", "col"),
            P("row", "col"),
            P(),
            P(),
            P(),
            P(),
            P(),
            P(),
            P(),
            P(),
        ),
        out_specs=P("sec", "row", "col"),
        check_vma=False,
    )
```
